256 devices in a mesh: az: 16 (over z_lo, x, core), tile: 16 (over y, z_hi).
Axes of the slice: x: 4, y: 4, z: 8 (z_hi: 4, z_lo: 2; z = z_hi * 2 + z_lo), core: 2. Of those that a mesh axis runs over, the one named last changes fastest.
Arguments:
- image: float32 [2, 8192, 2048], P(None, 'tile', 'az'), may hold values from -6 to 6
- tv_dual: float32 [2, 2, 8192, 2048], P(None, None, 'tile', 'az'), may hold values from -3 to 3
- data_dual: float32 [2, 1024, 64, 128], P(None, 'az', 'tile'), may hold values from -3 to 3
- echoes: bfloat16 [2, 1024, 64, 128], P(None, 'az', 'tile'), may hold values from -6 to 6
- row_steer: bfloat16 [2, 1024, 32, 256], P(None, None, 'tile'), may hold values from -0.375 to 0.375
- col_steer: float32 [2, 1024, 32, 16], P(None, None, 'tile'), may hold values from -1.5 to 1.5
- kernels: bfloat16 [8, 128, 128], replicated, may hold values from -0.5 to 0.5
- footprint: int32 [32, 16, 6], P(None, 'az'), may hold values from 0 to 63
- phase: int32 [32, 16, 6], P(None, 'az'), may hold values from 0 to 7
- aperture: int32 [1024], P('az'), may hold values from 0 to 1, as said below
Outputs:
- image_new: float32 [2, 8192, 2048], P(None, 'tile', 'az')
- tv_new: float32 [2, 2, 8192, 2048], P(None, None, 'tile', 'az')
- dual_new: float32 [2, 1024, 64, 128], P(None, 'az', 'tile')
The draws below stay inside these ranges and needn't reach their ends.
Inputs may be any that keep to these rules, and one draw needn't show every extreme that they name: 0 inside up to three gaps of 64 consecutive pulses each (wrapping around the aperture), 1 elsewhere.
All inputs are finite; a program needn't handle non-finite values.
Results may differ from the reference program's by a relative error of at most 0.0025.
The reference program's roundings to bfloat16 on the way count: a program that leaves them out, or rounds other values in their place, can miss the bound.
Values may be sent and summed in bfloat16 or wider, within the bound.
No kernel may reach another device: no remote copies, remote signals or barrier semaphores. Data moves between devices by JAX's collectives and lax.ppermute only.
A program may use at most 64 MiB of HBM per device.

```python
import jax
import jax.numpy as jnp
from jax import lax

RB = 128
NROW = 64
PB = 64
TH = 256
F = 6
NPH = 8
NPULSE = 1024
NBLK = 16
NTILES = 32
NY = 8192
NX = 2048


def draw_aperture(key, part):
    position = jnp.arange(NPULSE, dtype=jnp.int32)
    starts = jax.random.randint(key, (3,), 0, NPULSE, dtype=jnp.int32)
    gap_length = max(NPULSE // 16, 1)
    inside = (position[None, :] - starts[:, None]) % NPULSE < gap_length
    return jnp.where(jnp.any(inside, axis=0), 0, 1).astype(jnp.int32)


def place_ends(array, own_key, least, high):
    longest = array.shape.index(max(array.shape))
    spots = []
    for shift in (0, 1):
        where = [jax.random.randint(jax.random.fold_in(own_key, axis), (), 0, length) for axis, length in enumerate(array.shape)]
        where[longest] = (where[longest] + shift) % array.shape[longest]
        spots.append(tuple(where))
    return array.at[spots[0]].set(least).at[spots[1]].set(high)


def block_scale(rng, extent, cuts, low, largest):
    factor_of, own = 1.0, jax.random.fold_in(rng, 6)
    for dim, blocks in cuts:
        draws = jnp.exp(jax.random.uniform(jax.random.fold_in(own, dim), (blocks,), jnp.float32, low / len(cuts), largest / len(cuts)))
        factor_of = factor_of * jnp.repeat(draws, extent[dim] // blocks).reshape([-1 if axis == dim else 1 for axis in range(len(extent))])
    return factor_of


def gaussian(key, shape, deviation, limit, shards=(), kind=jnp.bfloat16):
    gain = block_scale(key, shape, shards, -0.22, 0.18) if shards else 1.0
    array = jax.random.normal(key, shape, jnp.float32) * deviation * gain
    return jnp.minimum(jnp.maximum(array, -limit), limit).astype(kind)


def setup_inputs(seed: int = 0) -> dict:
    seeds = jax.random.split(jax.random.key(seed), 11)
    return {
        "image": gaussian(seeds[0], (2, NY, NX), 1.0, 6.0, ((1, 16), (2, 16)), jnp.float32),
        "tv_dual": gaussian(seeds[1], (2, 2, NY, NX), 0.5, 3.0, ((2, 16), (3, 16)), jnp.float32),
        "data_dual": gaussian(seeds[2], (2, NPULSE, NROW, RB), 0.5, 3.0, ((1, 16), (2, 16)), jnp.float32),
        "echoes": gaussian(seeds[3], (2, NPULSE, NROW, RB), 1.0, 6.0, ((1, 16), (2, 16))),
        "row_steer": gaussian(seeds[4], (2, NPULSE, NTILES, TH), TH ** -0.5, 0.375, ((2, 16),)),
        "col_steer": gaussian(seeds[5], (2, NPULSE, NTILES, NBLK), NBLK ** -0.5, 1.5, ((2, 16),), jnp.float32),
        "kernels": gaussian(seeds[6], (NPH, RB, RB), RB ** -0.5, 0.5),
        "footprint": place_ends(jax.random.randint(seeds[7], (NTILES, NBLK, F), 0, NROW), jax.random.fold_in(seeds[7], 1), 0, NROW - 1).astype(jnp.int32),
        "phase": place_ends(jax.random.randint(seeds[8], (NTILES, NBLK, F), 0, NPH), jax.random.fold_in(seeds[8], 1), 0, NPH - 1).astype(jnp.int32),
        "aperture": draw_aperture(jax.random.fold_in(seeds[10], 71), 0),
    }


dual_step = 0.5
primal_step = 0.25
edge_limit = 1.5

def reference(image, tv_dual, data_dual, echoes, row_steer, col_steer, kernels, footprint, phase, aperture):
    highest = lax.Precision.HIGHEST
    image_b = image.astype(jnp.bfloat16).astype(jnp.float32)
    steer = row_steer.astype(jnp.float32)
    kern_all = kernels.astype(jnp.float32)
    row_ids = jnp.arange(NROW, dtype=jnp.int32)

    def tile_parts(index):
        steer_re = steer[0, :, index, :]
        steer_im = steer[1, :, index, :]
        col_re = col_steer[0, :, index, :]
        col_im = col_steer[1, :, index, :]
        kern = kern_all[phase[index]]
        onehot = (footprint[index][:, :, None] == row_ids[None, None, :]).astype(jnp.float32)
        return (steer_re, steer_im, col_re, col_im, kern, onehot)

    def forward_tile(index, total):
        steer_re, steer_im, col_re, col_im, kern, onehot = tile_parts(index)
        tile_img = lax.dynamic_slice_in_dim(image_b, index * TH, TH, 1)
        part_re = jnp.dot(steer_re, tile_img[0], precision=highest) - jnp.dot(steer_im, tile_img[1], precision=highest)
        part_im = jnp.dot(steer_re, tile_img[1], precision=highest) + jnp.dot(steer_im, tile_img[0], precision=highest)
        part_re = part_re.reshape(NPULSE, NBLK, RB)
        part_im = part_im.reshape(NPULSE, NBLK, RB)
        proj_re = lax.optimization_barrier(jnp.sum(col_re[:, :, None] * part_re - col_im[:, :, None] * part_im, axis=1))
        proj_im = lax.optimization_barrier(jnp.sum(col_re[:, :, None] * part_im + col_im[:, :, None] * part_re, axis=1))
        proj_b = jnp.stack([proj_re, proj_im]).astype(jnp.bfloat16).astype(jnp.float32).reshape(2, NBLK, PB, RB)
        placed = jnp.einsum('cbpu,bfuv->cbfpv', proj_b, kern, precision=highest)
        return total + jnp.einsum('cbfpv,bfk->cbpkv', placed, onehot, precision=highest)
    forward = lax.fori_loop(0, NTILES, forward_tile, jnp.zeros((2, NBLK, PB, NROW, RB), jnp.float32))
    forward = forward.reshape(2, NPULSE, NROW, RB)
    live = (aperture == 1)[None, :, None, None]
    dual_new = jnp.where(live, (data_dual + dual_step * (forward - echoes.astype(jnp.float32))) / (1.0 + dual_step), 0.0)
    dual_b = dual_new.astype(jnp.bfloat16).astype(jnp.float32).reshape(2, NBLK, PB, NROW, RB)

    def backward_tile(index):
        steer_re, steer_im, col_re, col_im, kern, onehot = tile_parts(index)
        chosen = jnp.einsum('cbpkv,bfk->cbfpv', dual_b, onehot, precision=highest)
        back = jnp.einsum('cbfpv,bfuv->cbpu', chosen, kern, precision=highest)
        back_b = back.astype(jnp.bfloat16).astype(jnp.float32).reshape(2, NPULSE, RB)
        back_re = back_b[0][:, None, :]
        back_im = back_b[1][:, None, :]
        weight_re = (col_re[:, :, None] * back_re + col_im[:, :, None] * back_im).astype(jnp.bfloat16).astype(jnp.float32)
        weight_im = (col_re[:, :, None] * back_im - col_im[:, :, None] * back_re).astype(jnp.bfloat16).astype(jnp.float32)
        weight_re = weight_re.reshape(NPULSE, NX)
        weight_im = weight_im.reshape(NPULSE, NX)
        grad_re = jnp.dot(steer_re.T, weight_re, precision=highest) + jnp.dot(steer_im.T, weight_im, precision=highest)
        grad_im = jnp.dot(steer_re.T, weight_im, precision=highest) - jnp.dot(steer_im.T, weight_re, precision=highest)
        return jnp.stack([grad_re, grad_im])
    adjoint = lax.map(backward_tile, jnp.arange(NTILES, dtype=jnp.int32))
    adjoint = jnp.transpose(adjoint, (1, 0, 2, 3)).reshape(2, NY, NX)
    zero_row = jnp.zeros((2, 1, NX), jnp.float32)
    zero_col = jnp.zeros((2, NY, 1), jnp.float32)
    grad_rows = jnp.concatenate([image[:, 1:, :] - image[:, :-1, :], zero_row], axis=1)
    grad_cols = jnp.concatenate([image[:, :, 1:] - image[:, :, :-1], zero_col], axis=2)
    moved = tv_dual + dual_step * jnp.stack([grad_rows, grad_cols])
    magnitude = jnp.sqrt(lax.optimization_barrier(jnp.sum(moved * moved, axis=(0, 1))))
    tv_new = moved / jnp.maximum(1.0, magnitude / edge_limit)
    rows_part = jnp.concatenate([tv_new[0][:, :-1, :], zero_row], axis=1)
    cols_part = jnp.concatenate([tv_new[1][:, :, :-1], zero_col], axis=2)
    divergence = rows_part - jnp.concatenate([zero_row, rows_part[:, :-1, :]], axis=1)
    divergence = divergence + cols_part - jnp.concatenate([zero_col, cols_part[:, :, :-1]], axis=2)
    image_new = image - primal_step * (adjoint - divergence)
    return (image_new, tv_new, dual_new)
```

```python
import jax
import jax.numpy as jnp
from jax import lax
from jax.sharding import PartitionSpec as P

dual_step = 0.5
primal_step = 0.25
edge_limit = 1.5


def padded_2(block, sides, width):
    for axis, dim in sides:
        count = lax.axis_size(axis)
        forward = [(i, i + 1) for i in range(count - 1)]
        backward = [(target, source) for source, target in forward]
        low = lax.ppermute(
            lax.slice_in_dim(block, block.shape[dim] - width, None, axis=dim), axis, forward
        )
        high = lax.ppermute(lax.slice_in_dim(block, 0, width, axis=dim), axis, backward)
        block = jnp.concatenate([low, block, high], axis=dim)
    return block


def on_device(
    image, tv_dual, data_dual, echoes, row_steer, col_steer, kernels, footprint, phase, aperture
):
    highest = lax.Precision.HIGHEST
    az_index = lax.axis_index("az")
    tile_index = lax.axis_index("tile")
    az_count = lax.axis_size("az")
    tile_count = lax.axis_size("tile")
    strip_rows = image.shape[1]
    columns = image.shape[2]
    tiles_dev = row_steer.shape[2]
    tile_rows = row_steer.shape[3]
    rows_dev = data_dual.shape[2]
    range_rows = rows_dev * tile_count
    foot_block = footprint[:, 0, :]
    phase_block = phase[:, 0, :]
    foot_mine = lax.dynamic_slice_in_dim(foot_block, tile_index * tiles_dev, tiles_dev, 0)
    phase_mine = lax.dynamic_slice_in_dim(phase_block, tile_index * tiles_dev, tiles_dev, 0)
    steer_re = row_steer[0]
    steer_im = row_steer[1]
    col_mine = lax.dynamic_slice_in_dim(col_steer, az_index, 1, 3)[..., 0]
    image_b = image.astype(jnp.bfloat16).reshape(2, tiles_dev, tile_rows, columns)
    part_sre = steer_re
    part_sim = steer_im
    weight_re = col_mine[0][..., None]
    weight_im = col_mine[1][..., None]
    prod_re = jnp.einsum("pjh,jhu->pju", part_sre, image_b[0], preferred_element_type=jnp.float32)
    prod_re = prod_re - jnp.einsum(
        "pjh,jhu->pju", part_sim, image_b[1], preferred_element_type=jnp.float32
    )
    prod_im = jnp.einsum("pjh,jhu->pju", part_sre, image_b[1], preferred_element_type=jnp.float32)
    prod_im = prod_im + jnp.einsum(
        "pjh,jhu->pju", part_sim, image_b[0], preferred_element_type=jnp.float32
    )
    real_part = weight_re * prod_re - weight_im * prod_im
    imag_part = weight_re * prod_im + weight_im * prod_re
    summed = lax.psum_scatter(
        jnp.stack([real_part, imag_part], axis=0), "az", scatter_dimension=1, tiled=True
    )
    projection_b = jnp.transpose(summed, (2, 1, 0, 3)).astype(jnp.bfloat16)
    all_proj = lax.all_gather(projection_b, "tile", axis=0, tiled=True)
    phase_ids = jnp.arange(kernels.shape[0], dtype=jnp.int32)
    my_rows = tile_index * rows_dev + jnp.arange(rows_dev, dtype=jnp.int32)
    hits = (foot_block[:, :, None, None] == my_rows[None, None, :, None]) & (
        phase_block[:, :, None, None] == phase_ids[None, None, None, :]
    )
    counts = jnp.sum(hits.astype(jnp.int32), axis=1).astype(jnp.bfloat16)
    grouped = jnp.einsum(
        "jkq,jpcu->kqpcu", counts, all_proj, preferred_element_type=jnp.float32
    )
    forward = jnp.einsum(
        "kqpcu,quv->cpkv", grouped, kernels.astype(jnp.float32), precision=highest
    )
    kern_mine = kernels[phase_mine]
    live = (aperture == 1)[None, :, None, None]
    dual_new = jnp.where(
        live,
        (data_dual + dual_step * (forward - echoes.astype(jnp.float32))) / (1.0 + dual_step),
        0.0,
    )
    dual_b = dual_new.astype(jnp.bfloat16)
    all_rows = lax.all_gather(dual_b, "tile", axis=2, tiled=True)
    chosen = jnp.take(all_rows, foot_mine, axis=2)
    back = jnp.einsum("cpjfv,jfuv->cjpu", chosen, kern_mine, preferred_element_type=jnp.float32)
    back_b = back.astype(jnp.bfloat16)
    piece = lax.all_gather(back_b, "az", axis=2, tiled=True)
    weight_re = col_mine[0].T[..., None]
    weight_im = col_mine[1].T[..., None]
    back_re = piece[0].astype(jnp.float32)
    back_im = piece[1].astype(jnp.float32)
    mixed_re = (weight_re * back_re + weight_im * back_im).astype(jnp.bfloat16)
    mixed_im = (weight_re * back_im - weight_im * back_re).astype(jnp.bfloat16)
    part_sre = steer_re
    part_sim = steer_im
    grad_re = jnp.einsum("pjh,jpu->jhu", part_sre, mixed_re, preferred_element_type=jnp.float32)
    grad_re = grad_re + jnp.einsum(
        "pjh,jpu->jhu", part_sim, mixed_im, preferred_element_type=jnp.float32
    )
    grad_im = jnp.einsum("pjh,jpu->jhu", part_sre, mixed_im, preferred_element_type=jnp.float32)
    grad_im = grad_im - jnp.einsum(
        "pjh,jpu->jhu", part_sim, mixed_re, preferred_element_type=jnp.float32
    )
    adjoint = jnp.stack([grad_re, grad_im])
    adjoint = adjoint.reshape(2, strip_rows, columns)
    stacked = jnp.concatenate([image, tv_dual.reshape(4, strip_rows, columns)], axis=0)
    padded = padded_2(stacked, (("az", 2), ("tile", 1)), 1)
    image_pad = padded[:2]
    dual_pad = padded[2:].reshape(2, 2, strip_rows + 2, columns + 2)
    total_rows = tile_count * strip_rows
    total_cols = az_count * columns
    global_row = tile_index * strip_rows - 1 + jnp.arange(strip_rows + 1, dtype=jnp.int32)
    global_col = az_index * columns - 1 + jnp.arange(columns + 1, dtype=jnp.int32)
    centre = image_pad[:, : strip_rows + 1, : columns + 1]
    grad_rows = image_pad[:, 1 : strip_rows + 2, : columns + 1] - centre
    grad_rows = jnp.where((global_row < total_rows - 1)[None, :, None], grad_rows, 0.0)
    grad_cols = image_pad[:, : strip_rows + 1, 1 : columns + 2] - centre
    grad_cols = jnp.where((global_col < total_cols - 1)[None, None, :], grad_cols, 0.0)
    moved = dual_pad[:, :, : strip_rows + 1, : columns + 1] + dual_step * jnp.stack(
        [grad_rows, grad_cols]
    )
    magnitude = jnp.sqrt(jnp.sum(moved * moved, axis=(0, 1)))
    projected = moved / jnp.maximum(1.0, magnitude / edge_limit)
    inside = (global_row >= 0)[:, None] & (global_col >= 0)[None, :]
    projected = jnp.where(inside[None, None], projected, 0.0)
    rows_part = jnp.where((global_row < total_rows - 1)[None, :, None], projected[0], 0.0)
    cols_part = jnp.where((global_col < total_cols - 1)[None, None, :], projected[1], 0.0)
    divergence = (
        rows_part[:, 1:, 1:] - rows_part[:, :-1, 1:] + cols_part[:, 1:, 1:] - cols_part[:, 1:, :-1]
    )
    image_new = image - primal_step * (adjoint - divergence)
    tv_new = projected[:, :, 1:, 1:]
    return (image_new, tv_new, dual_new)


def solution(mesh):
    in_specs = (
        P(None, "tile", "az"),
        P(None, None, "tile", "az"),
        P(None, "az", "tile", None),
        P(None, "az", "tile", None),
        P(None, None, "tile", None),
        P(None, None, "tile", None),
        P(),
        P(None, "az", None),
        P(None, "az", None),
        P("az"),
    )
    out_specs = (P(None, "tile", "az"), P(None, None, "tile", "az"), P(None, "az", "tile", None))
    return jax.shard_map(
        on_device, mesh=mesh, in_specs=in_specs, out_specs=out_specs, check_vma=False
    )
```

```python
import jax
import jax.numpy as jnp
from jax import lax
from jax.sharding import PartitionSpec as P

dual_step = 0.5
primal_step = 0.25
edge_limit = 1.5


def padded_2(block, sides, width):
    for axis, dim in sides:
        count = lax.axis_size(axis)
        forward = [(i, i + 1) for i in range(count - 1)]
        backward = [(target, source) for source, target in forward]
        low = lax.ppermute(
            lax.slice_in_dim(block, block.shape[dim] - width, None, axis=dim), axis, forward
        )
        high = lax.ppermute(lax.slice_in_dim(block, 0, width, axis=dim), axis, backward)
        block = jnp.concatenate([low, block, high], axis=dim)
    return block


def halving_sum(blocks, axis, bits):
    me = lax.axis_index(axis)
    count = lax.axis_size(axis)
    order = [count >> (level + 1) for level in range(count.bit_length() - 1)]
    blocks = blocks.reshape(*([2] * len(order)), *blocks.shape[1:])
    for bit in bits:
        place = order.index(bit)
        order.pop(place)
        mine = (me // bit) % 2
        keep = lax.dynamic_index_in_dim(blocks, mine, place, keepdims=False)
        send = lax.dynamic_index_in_dim(blocks, 1 - mine, place, keepdims=False)
        pairs = [(i, i ^ bit) for i in range(count)]
        blocks = keep + lax.ppermute(send, axis, pairs)
    return blocks


def on_device(
    image, tv_dual, data_dual, echoes, row_steer, col_steer, kernels, footprint, phase, aperture
):
    highest = lax.Precision.HIGHEST
    az_index = lax.axis_index("az")
    tile_index = lax.axis_index("tile")
    az_count = lax.axis_size("az")
    tile_count = lax.axis_size("tile")
    strip_rows = image.shape[1]
    columns = image.shape[2]
    tiles_dev = row_steer.shape[2]
    tile_rows = row_steer.shape[3]
    rows_dev = data_dual.shape[2]
    range_rows = rows_dev * tile_count
    foot_block = footprint[:, 0, :]
    phase_block = phase[:, 0, :]
    foot_mine = lax.dynamic_slice_in_dim(foot_block, tile_index * tiles_dev, tiles_dev, 0)
    phase_mine = lax.dynamic_slice_in_dim(phase_block, tile_index * tiles_dev, tiles_dev, 0)
    steer_re = row_steer[0]
    steer_im = row_steer[1]
    col_mine = lax.dynamic_slice_in_dim(col_steer, az_index, 1, 3)[..., 0]
    image_b = image.astype(jnp.bfloat16).reshape(2, tiles_dev, tile_rows, columns)
    part_sre = steer_re
    part_sim = steer_im
    weight_re = col_mine[0][..., None]
    weight_im = col_mine[1][..., None]
    prod_re = jnp.einsum("pjh,jhu->pju", part_sre, image_b[0], preferred_element_type=jnp.float32)
    prod_re = prod_re - jnp.einsum(
        "pjh,jhu->pju", part_sim, image_b[1], preferred_element_type=jnp.float32
    )
    prod_im = jnp.einsum("pjh,jhu->pju", part_sre, image_b[1], preferred_element_type=jnp.float32)
    prod_im = prod_im + jnp.einsum(
        "pjh,jhu->pju", part_sim, image_b[0], preferred_element_type=jnp.float32
    )
    real_part = weight_re * prod_re - weight_im * prod_im
    imag_part = weight_re * prod_im + weight_im * prod_re
    parts = jnp.stack([real_part, imag_part], axis=0).reshape(2, az_count, -1, tiles_dev, columns)
    summed = halving_sum(jnp.moveaxis(parts, 1, 0), "az", (1, 8, 2, 4))
    projection_b = jnp.transpose(summed, (2, 1, 0, 3)).astype(jnp.bfloat16)
    all_proj = lax.all_gather(projection_b, "tile", axis=0, tiled=True)
    phase_ids = jnp.arange(kernels.shape[0], dtype=jnp.int32)
    my_rows = tile_index * rows_dev + jnp.arange(rows_dev, dtype=jnp.int32)
    hits = (foot_block[:, :, None, None] == my_rows[None, None, :, None]) & (
        phase_block[:, :, None, None] == phase_ids[None, None, None, :]
    )
    counts = jnp.sum(hits.astype(jnp.int32), axis=1).astype(jnp.bfloat16)
    grouped = jnp.einsum(
        "jkq,jpcu->kqpcu", counts, all_proj, preferred_element_type=jnp.float32
    )
    forward = jnp.einsum(
        "kqpcu,quv->cpkv", grouped, kernels.astype(jnp.float32), precision=highest
    )
    kern_mine = kernels[phase_mine]
    live = (aperture == 1)[None, :, None, None]
    dual_new = jnp.where(
        live,
        (data_dual + dual_step * (forward - echoes.astype(jnp.float32))) / (1.0 + dual_step),
        0.0,
    )
    dual_b = dual_new.astype(jnp.bfloat16)
    all_rows = lax.all_gather(dual_b, "tile", axis=2, tiled=True)
    chosen = jnp.take(all_rows, foot_mine, axis=2)
    back = jnp.einsum("cpjfv,jfuv->cjpu", chosen, kern_mine, preferred_element_type=jnp.float32)
    back_b = back.astype(jnp.bfloat16)
    piece = lax.all_gather(back_b, "az", axis=2, tiled=True)
    weight_re = col_mine[0].T[..., None]
    weight_im = col_mine[1].T[..., None]
    back_re = piece[0].astype(jnp.float32)
    back_im = piece[1].astype(jnp.float32)
    mixed_re = (weight_re * back_re + weight_im * back_im).astype(jnp.bfloat16)
    mixed_im = (weight_re * back_im - weight_im * back_re).astype(jnp.bfloat16)
    part_sre = steer_re
    part_sim = steer_im
    grad_re = jnp.einsum("pjh,jpu->jhu", part_sre, mixed_re, preferred_element_type=jnp.float32)
    grad_re = grad_re + jnp.einsum(
        "pjh,jpu->jhu", part_sim, mixed_im, preferred_element_type=jnp.float32
    )
    grad_im = jnp.einsum("pjh,jpu->jhu", part_sre, mixed_im, preferred_element_type=jnp.float32)
    grad_im = grad_im - jnp.einsum(
        "pjh,jpu->jhu", part_sim, mixed_re, preferred_element_type=jnp.float32
    )
    adjoint = jnp.stack([grad_re, grad_im])
    adjoint = adjoint.reshape(2, strip_rows, columns)
    stacked = jnp.concatenate([image, tv_dual.reshape(4, strip_rows, columns)], axis=0)
    padded = padded_2(stacked, (("az", 2), ("tile", 1)), 1)
    image_pad = padded[:2]
    dual_pad = padded[2:].reshape(2, 2, strip_rows + 2, columns + 2)
    total_rows = tile_count * strip_rows
    total_cols = az_count * columns
    global_row = tile_index * strip_rows - 1 + jnp.arange(strip_rows + 1, dtype=jnp.int32)
    global_col = az_index * columns - 1 + jnp.arange(columns + 1, dtype=jnp.int32)
    centre = image_pad[:, : strip_rows + 1, : columns + 1]
    grad_rows = image_pad[:, 1 : strip_rows + 2, : columns + 1] - centre
    grad_rows = jnp.where((global_row < total_rows - 1)[None, :, None], grad_rows, 0.0)
    grad_cols = image_pad[:, : strip_rows + 1, 1 : columns + 2] - centre
    grad_cols = jnp.where((global_col < total_cols - 1)[None, None, :], grad_cols, 0.0)
    moved = dual_pad[:, :, : strip_rows + 1, : columns + 1] + dual_step * jnp.stack(
        [grad_rows, grad_cols]
    )
    magnitude = jnp.sqrt(jnp.sum(moved * moved, axis=(0, 1)))
    projected = moved / jnp.maximum(1.0, magnitude / edge_limit)
    inside = (global_row >= 0)[:, None] & (global_col >= 0)[None, :]
    projected = jnp.where(inside[None, None], projected, 0.0)
    rows_part = jnp.where((global_row < total_rows - 1)[None, :, None], projected[0], 0.0)
    cols_part = jnp.where((global_col < total_cols - 1)[None, None, :], projected[1], 0.0)
    divergence = (
        rows_part[:, 1:, 1:] - rows_part[:, :-1, 1:] + cols_part[:, 1:, 1:] - cols_part[:, 1:, :-1]
    )
    image_new = image - primal_step * (adjoint - divergence)
    tv_new = projected[:, :, 1:, 1:]
    return (image_new, tv_new, dual_new)


def solution(mesh):
    in_specs = (
        P(None, "tile", "az"),
        P(None, None, "tile", "az"),
        P(None, "az", "tile", None),
        P(None, "az", "tile", None),
        P(None, None, "tile", None),
        P(None, None, "tile", None),
        P(),
        P(None, "az", None),
        P(None, "az", None),
        P("az"),
    )
    out_specs = (P(None, "tile", "az"), P(None, None, "tile", "az"), P(None, "az", "tile", None))
    return jax.shard_map(
        on_device, mesh=mesh, in_specs=in_specs, out_specs=out_specs, check_vma=False
    )
```

```python
import jax
import jax.numpy as jnp
from jax import lax
from jax.sharding import PartitionSpec as P

dual_step = 0.5
primal_step = 0.25
edge_limit = 1.5


def padded_2(block, sides, width):
    for axis, dim in sides:
        count = lax.axis_size(axis)
        forward = [(i, i + 1) for i in range(count - 1)]
        backward = [(target, source) for source, target in forward]
        low = lax.ppermute(
            lax.slice_in_dim(block, block.shape[dim] - width, None, axis=dim), axis, forward
        )
        high = lax.ppermute(lax.slice_in_dim(block, 0, width, axis=dim), axis, backward)
        block = jnp.concatenate([low, block, high], axis=dim)
    return block


def halving_sum(blocks, axis, bits):
    me = lax.axis_index(axis)
    count = lax.axis_size(axis)
    order = [count >> (level + 1) for level in range(count.bit_length() - 1)]
    blocks = blocks.reshape(*([2] * len(order)), *blocks.shape[1:])
    for bit in bits:
        place = order.index(bit)
        order.pop(place)
        mine = (me // bit) % 2
        keep = lax.dynamic_index_in_dim(blocks, mine, place, keepdims=False)
        send = lax.dynamic_index_in_dim(blocks, 1 - mine, place, keepdims=False)
        pairs = [(i, i ^ bit) for i in range(count)]
        blocks = keep + lax.ppermute(send, axis, pairs)
    return blocks


def doubling_gather(block, axis, bits):
    me = lax.axis_index(axis)
    count = lax.axis_size(axis)
    done = []
    for bit in bits:
        mine = (me // bit) % 2
        pairs = [(i, i ^ bit) for i in range(count)]
        got = lax.ppermute(block, axis, pairs)
        place = sum(1 for other in done if other > bit)
        low = jnp.where(mine == 0, block, got)
        high = jnp.where(mine == 0, got, block)
        block = jnp.stack([low, high], axis=place)
        done.append(bit)
    return block.reshape(count, *block.shape[len(bits):])


def on_device(
    image, tv_dual, data_dual, echoes, row_steer, col_steer, kernels, footprint, phase, aperture
):
    highest = lax.Precision.HIGHEST
    az_index = lax.axis_index("az")
    tile_index = lax.axis_index("tile")
    az_count = lax.axis_size("az")
    tile_count = lax.axis_size("tile")
    strip_rows = image.shape[1]
    columns = image.shape[2]
    tiles_dev = row_steer.shape[2]
    tile_rows = row_steer.shape[3]
    rows_dev = data_dual.shape[2]
    range_rows = rows_dev * tile_count
    foot_block = footprint[:, 0, :]
    phase_block = phase[:, 0, :]
    foot_mine = lax.dynamic_slice_in_dim(foot_block, tile_index * tiles_dev, tiles_dev, 0)
    phase_mine = lax.dynamic_slice_in_dim(phase_block, tile_index * tiles_dev, tiles_dev, 0)
    steer_re = row_steer[0]
    steer_im = row_steer[1]
    col_mine = lax.dynamic_slice_in_dim(col_steer, az_index, 1, 3)[..., 0]
    image_b = image.astype(jnp.bfloat16).reshape(2, tiles_dev, tile_rows, columns)
    part_sre = steer_re
    part_sim = steer_im
    weight_re = col_mine[0][..., None]
    weight_im = col_mine[1][..., None]
    prod_re = jnp.einsum("pjh,jhu->pju", part_sre, image_b[0], preferred_element_type=jnp.float32)
    prod_re = prod_re - jnp.einsum(
        "pjh,jhu->pju", part_sim, image_b[1], preferred_element_type=jnp.float32
    )
    prod_im = jnp.einsum("pjh,jhu->pju", part_sre, image_b[1], preferred_element_type=jnp.float32)
    prod_im = prod_im + jnp.einsum(
        "pjh,jhu->pju", part_sim, image_b[0], preferred_element_type=jnp.float32
    )
    real_part = weight_re * prod_re - weight_im * prod_im
    imag_part = weight_re * prod_im + weight_im * prod_re
    parts = jnp.stack([real_part, imag_part], axis=0).reshape(2, az_count, -1, tiles_dev, columns)
    summed = halving_sum(jnp.moveaxis(parts, 1, 0), "az", (1, 8, 2, 4))
    projection_b = jnp.transpose(summed, (2, 1, 0, 3)).astype(jnp.bfloat16)
    all_proj = doubling_gather(projection_b, "tile", (2, 1, 8, 4))
    all_proj = all_proj.reshape(-1, *all_proj.shape[2:])
    phase_ids = jnp.arange(kernels.shape[0], dtype=jnp.int32)
    my_rows = tile_index * rows_dev + jnp.arange(rows_dev, dtype=jnp.int32)
    hits = (foot_block[:, :, None, None] == my_rows[None, None, :, None]) & (
        phase_block[:, :, None, None] == phase_ids[None, None, None, :]
    )
    counts = jnp.sum(hits.astype(jnp.int32), axis=1).astype(jnp.bfloat16)
    grouped = jnp.einsum(
        "jkq,jpcu->kqpcu", counts, all_proj, preferred_element_type=jnp.float32
    )
    forward = jnp.einsum(
        "kqpcu,quv->cpkv", grouped, kernels.astype(jnp.float32), precision=highest
    )
    kern_mine = kernels[phase_mine]
    live = (aperture == 1)[None, :, None, None]
    dual_new = jnp.where(
        live,
        (data_dual + dual_step * (forward - echoes.astype(jnp.float32))) / (1.0 + dual_step),
        0.0,
    )
    dual_b = dual_new.astype(jnp.bfloat16)
    all_rows = doubling_gather(jnp.moveaxis(dual_b, 2, 0), "tile", (2, 1, 8, 4))
    all_rows = jnp.moveaxis(all_rows.reshape(-1, *all_rows.shape[2:]), 0, 2)
    chosen = jnp.take(all_rows, foot_mine, axis=2)
    back = jnp.einsum("cpjfv,jfuv->cjpu", chosen, kern_mine, preferred_element_type=jnp.float32)
    back_b = back.astype(jnp.bfloat16)
    piece = doubling_gather(jnp.moveaxis(back_b, 2, 0), "az", (4, 8, 2, 1))
    piece = jnp.moveaxis(piece.reshape(-1, *piece.shape[2:]), 0, 2)
    weight_re = col_mine[0].T[..., None]
    weight_im = col_mine[1].T[..., None]
    back_re = piece[0].astype(jnp.float32)
    back_im = piece[1].astype(jnp.float32)
    mixed_re = (weight_re * back_re + weight_im * back_im).astype(jnp.bfloat16)
    mixed_im = (weight_re * back_im - weight_im * back_re).astype(jnp.bfloat16)
    part_sre = steer_re
    part_sim = steer_im
    grad_re = jnp.einsum("pjh,jpu->jhu", part_sre, mixed_re, preferred_element_type=jnp.float32)
    grad_re = grad_re + jnp.einsum(
        "pjh,jpu->jhu", part_sim, mixed_im, preferred_element_type=jnp.float32
    )
    grad_im = jnp.einsum("pjh,jpu->jhu", part_sre, mixed_im, preferred_element_type=jnp.float32)
    grad_im = grad_im - jnp.einsum(
        "pjh,jpu->jhu", part_sim, mixed_re, preferred_element_type=jnp.float32
    )
    adjoint = jnp.stack([grad_re, grad_im])
    adjoint = adjoint.reshape(2, strip_rows, columns)
    stacked = jnp.concatenate([image, tv_dual.reshape(4, strip_rows, columns)], axis=0)
    padded = padded_2(stacked, (("az", 2), ("tile", 1)), 1)
    image_pad = padded[:2]
    dual_pad = padded[2:].reshape(2, 2, strip_rows + 2, columns + 2)
    total_rows = tile_count * strip_rows
    total_cols = az_count * columns
    global_row = tile_index * strip_rows - 1 + jnp.arange(strip_rows + 1, dtype=jnp.int32)
    global_col = az_index * columns - 1 + jnp.arange(columns + 1, dtype=jnp.int32)
    centre = image_pad[:, : strip_rows + 1, : columns + 1]
    grad_rows = image_pad[:, 1 : strip_rows + 2, : columns + 1] - centre
    grad_rows = jnp.where((global_row < total_rows - 1)[None, :, None], grad_rows, 0.0)
    grad_cols = image_pad[:, : strip_rows + 1, 1 : columns + 2] - centre
    grad_cols = jnp.where((global_col < total_cols - 1)[None, None, :], grad_cols, 0.0)
    moved = dual_pad[:, :, : strip_rows + 1, : columns + 1] + dual_step * jnp.stack(
        [grad_rows, grad_cols]
    )
    magnitude = jnp.sqrt(jnp.sum(moved * moved, axis=(0, 1)))
    projected = moved / jnp.maximum(1.0, magnitude / edge_limit)
    inside = (global_row >= 0)[:, None] & (global_col >= 0)[None, :]
    projected = jnp.where(inside[None, None], projected, 0.0)
    rows_part = jnp.where((global_row < total_rows - 1)[None, :, None], projected[0], 0.0)
    cols_part = jnp.where((global_col < total_cols - 1)[None, None, :], projected[1], 0.0)
    divergence = (
        rows_part[:, 1:, 1:] - rows_part[:, :-1, 1:] + cols_part[:, 1:, 1:] - cols_part[:, 1:, :-1]
    )
    image_new = image - primal_step * (adjoint - divergence)
    tv_new = projected[:, :, 1:, 1:]
    return (image_new, tv_new, dual_new)


def solution(mesh):
    in_specs = (
        P(None, "tile", "az"),
        P(None, None, "tile", "az"),
        P(None, "az", "tile", None),
        P(None, "az", "tile", None),
        P(None, None, "tile", None),
        P(None, None, "tile", None),
        P(),
        P(None, "az", None),
        P(None, "az", None),
        P("az"),
    )
    out_specs = (P(None, "tile", "az"), P(None, None, "tile", "az"), P(None, "az", "tile", None))
    return jax.shard_map(
        on_device, mesh=mesh, in_specs=in_specs, out_specs=out_specs, check_vma=False
    )
```

```python
import jax
import jax.numpy as jnp
from jax import lax
from jax.sharding import PartitionSpec as P

dual_step = 0.5
primal_step = 0.25
edge_limit = 1.5


def padded_2(block, sides, width):
    for axis, dim in sides:
        count = lax.axis_size(axis)
        forward = [(i, i + 1) for i in range(count - 1)]
        backward = [(target, source) for source, target in forward]
        low = lax.ppermute(
            lax.slice_in_dim(block, block.shape[dim] - width, None, axis=dim), axis, forward
        )
        high = lax.ppermute(lax.slice_in_dim(block, 0, width, axis=dim), axis, backward)
        block = jnp.concatenate([low, block, high], axis=dim)
    return block


def halving_sum(blocks, axis, bits):
    me = lax.axis_index(axis)
    count = lax.axis_size(axis)
    order = [count >> (level + 1) for level in range(count.bit_length() - 1)]
    blocks = blocks.reshape(*([2] * len(order)), *blocks.shape[1:])
    for bit in bits:
        place = order.index(bit)
        order.pop(place)
        mine = (me // bit) % 2
        keep = lax.dynamic_index_in_dim(blocks, mine, place, keepdims=False)
        send = lax.dynamic_index_in_dim(blocks, 1 - mine, place, keepdims=False)
        pairs = [(i, i ^ bit) for i in range(count)]
        blocks = keep + lax.ppermute(send, axis, pairs)
    return blocks


def doubling_gather(block, axis, bits):
    me = lax.axis_index(axis)
    count = lax.axis_size(axis)
    done = []
    for bit in bits:
        mine = (me // bit) % 2
        pairs = [(i, i ^ bit) for i in range(count)]
        got = lax.ppermute(block, axis, pairs)
        place = sum(1 for other in done if other > bit)
        low = jnp.where(mine == 0, block, got)
        high = jnp.where(mine == 0, got, block)
        block = jnp.stack([low, high], axis=place)
        done.append(bit)
    return block.reshape(count, *block.shape[len(bits):])


def swap_sum(blocks, axis):
    return jnp.sum(lax.all_to_all(blocks, axis, 0, 0, tiled=True), axis=0)


def swap_gather(block, axis):
    count = lax.axis_size(axis)
    spread = jnp.broadcast_to(block[None], (count, *block.shape))
    return lax.all_to_all(spread, axis, 0, 0, tiled=True)


def on_device(
    image, tv_dual, data_dual, echoes, row_steer, col_steer, kernels, footprint, phase, aperture
):
    highest = lax.Precision.HIGHEST
    az_index = lax.axis_index("az")
    tile_index = lax.axis_index("tile")
    az_count = lax.axis_size("az")
    tile_count = lax.axis_size("tile")
    strip_rows = image.shape[1]
    columns = image.shape[2]
    tiles_dev = row_steer.shape[2]
    tile_rows = row_steer.shape[3]
    rows_dev = data_dual.shape[2]
    range_rows = rows_dev * tile_count
    foot_block = footprint[:, 0, :]
    phase_block = phase[:, 0, :]
    foot_mine = lax.dynamic_slice_in_dim(foot_block, tile_index * tiles_dev, tiles_dev, 0)
    phase_mine = lax.dynamic_slice_in_dim(phase_block, tile_index * tiles_dev, tiles_dev, 0)
    steer_re = row_steer[0]
    steer_im = row_steer[1]
    col_mine = lax.dynamic_slice_in_dim(col_steer, az_index, 1, 3)[..., 0]
    image_b = image.astype(jnp.bfloat16).reshape(2, tiles_dev, tile_rows, columns)
    part_sre = steer_re
    part_sim = steer_im
    weight_re = col_mine[0][..., None]
    weight_im = col_mine[1][..., None]
    prod_re = jnp.einsum("pjh,jhu->pju", part_sre, image_b[0], preferred_element_type=jnp.float32)
    prod_re = prod_re - jnp.einsum(
        "pjh,jhu->pju", part_sim, image_b[1], preferred_element_type=jnp.float32
    )
    prod_im = jnp.einsum("pjh,jhu->pju", part_sre, image_b[1], preferred_element_type=jnp.float32)
    prod_im = prod_im + jnp.einsum(
        "pjh,jhu->pju", part_sim, image_b[0], preferred_element_type=jnp.float32
    )
    real_part = weight_re * prod_re - weight_im * prod_im
    imag_part = weight_re * prod_im + weight_im * prod_re
    parts = jnp.stack([real_part, imag_part], axis=0).reshape(2, az_count, -1, tiles_dev, columns)
    summed = swap_sum(jnp.moveaxis(parts, 1, 0), "az")
    projection_b = jnp.transpose(summed, (2, 1, 0, 3)).astype(jnp.bfloat16)
    all_proj = swap_gather(projection_b, "tile")
    all_proj = all_proj.reshape(-1, *all_proj.shape[2:])
    phase_ids = jnp.arange(kernels.shape[0], dtype=jnp.int32)
    my_rows = tile_index * rows_dev + jnp.arange(rows_dev, dtype=jnp.int32)
    hits = (foot_block[:, :, None, None] == my_rows[None, None, :, None]) & (
        phase_block[:, :, None, None] == phase_ids[None, None, None, :]
    )
    counts = jnp.sum(hits.astype(jnp.int32), axis=1).astype(jnp.bfloat16)
    grouped = jnp.einsum(
        "jkq,jpcu->kqpcu", counts, all_proj, preferred_element_type=jnp.float32
    )
    forward = jnp.einsum(
        "kqpcu,quv->cpkv", grouped, kernels.astype(jnp.float32), precision=highest
    )
    kern_mine = kernels[phase_mine]
    live = (aperture == 1)[None, :, None, None]
    dual_new = jnp.where(
        live,
        (data_dual + dual_step * (forward - echoes.astype(jnp.float32))) / (1.0 + dual_step),
        0.0,
    )
    dual_b = dual_new.astype(jnp.bfloat16)
    all_rows = swap_gather(jnp.moveaxis(dual_b, 2, 0), "tile")
    all_rows = jnp.moveaxis(all_rows.reshape(-1, *all_rows.shape[2:]), 0, 2)
    chosen = jnp.take(all_rows, foot_mine, axis=2)
    back = jnp.einsum("cpjfv,jfuv->cjpu", chosen, kern_mine, preferred_element_type=jnp.float32)
    back_b = back.astype(jnp.bfloat16)
    piece = swap_gather(jnp.moveaxis(back_b, 2, 0), "az")
    piece = jnp.moveaxis(piece.reshape(-1, *piece.shape[2:]), 0, 2)
    weight_re = col_mine[0].T[..., None]
    weight_im = col_mine[1].T[..., None]
    back_re = piece[0].astype(jnp.float32)
    back_im = piece[1].astype(jnp.float32)
    mixed_re = (weight_re * back_re + weight_im * back_im).astype(jnp.bfloat16)
    mixed_im = (weight_re * back_im - weight_im * back_re).astype(jnp.bfloat16)
    part_sre = steer_re
    part_sim = steer_im
    grad_re = jnp.einsum("pjh,jpu->jhu", part_sre, mixed_re, preferred_element_type=jnp.float32)
    grad_re = grad_re + jnp.einsum(
        "pjh,jpu->jhu", part_sim, mixed_im, preferred_element_type=jnp.float32
    )
    grad_im = jnp.einsum("pjh,jpu->jhu", part_sre, mixed_im, preferred_element_type=jnp.float32)
    grad_im = grad_im - jnp.einsum(
        "pjh,jpu->jhu", part_sim, mixed_re, preferred_element_type=jnp.float32
    )
    adjoint = jnp.stack([grad_re, grad_im])
    adjoint = adjoint.reshape(2, strip_rows, columns)
    stacked = jnp.concatenate([image, tv_dual.reshape(4, strip_rows, columns)], axis=0)
    padded = padded_2(stacked, (("az", 2), ("tile", 1)), 1)
    image_pad = padded[:2]
    dual_pad = padded[2:].reshape(2, 2, strip_rows + 2, columns + 2)
    total_rows = tile_count * strip_rows
    total_cols = az_count * columns
    global_row = tile_index * strip_rows - 1 + jnp.arange(strip_rows + 1, dtype=jnp.int32)
    global_col = az_index * columns - 1 + jnp.arange(columns + 1, dtype=jnp.int32)
    centre = image_pad[:, : strip_rows + 1, : columns + 1]
    grad_rows = image_pad[:, 1 : strip_rows + 2, : columns + 1] - centre
    grad_rows = jnp.where((global_row < total_rows - 1)[None, :, None], grad_rows, 0.0)
    grad_cols = image_pad[:, : strip_rows + 1, 1 : columns + 2] - centre
    grad_cols = jnp.where((global_col < total_cols - 1)[None, None, :], grad_cols, 0.0)
    moved = dual_pad[:, :, : strip_rows + 1, : columns + 1] + dual_step * jnp.stack(
        [grad_rows, grad_cols]
    )
    magnitude = jnp.sqrt(jnp.sum(moved * moved, axis=(0, 1)))
    projected = moved / jnp.maximum(1.0, magnitude / edge_limit)
    inside = (global_row >= 0)[:, None] & (global_col >= 0)[None, :]
    projected = jnp.where(inside[None, None], projected, 0.0)
    rows_part = jnp.where((global_row < total_rows - 1)[None, :, None], projected[0], 0.0)
    cols_part = jnp.where((global_col < total_cols - 1)[None, None, :], projected[1], 0.0)
    divergence = (
        rows_part[:, 1:, 1:] - rows_part[:, :-1, 1:] + cols_part[:, 1:, 1:] - cols_part[:, 1:, :-1]
    )
    image_new = image - primal_step * (adjoint - divergence)
    tv_new = projected[:, :, 1:, 1:]
    return (image_new, tv_new, dual_new)


def solution(mesh):
    in_specs = (
        P(None, "tile", "az"),
        P(None, None, "tile", "az"),
        P(None, "az", "tile", None),
        P(None, "az", "tile", None),
        P(None, None, "tile", None),
        P(None, None, "tile", None),
        P(),
        P(None, "az", None),
        P(None, "az", None),
        P("az"),
    )
    out_specs = (P(None, "tile", "az"), P(None, None, "tile", "az"), P(None, "az", "tile", None))
    return jax.shard_map(
        on_device, mesh=mesh, in_specs=in_specs, out_specs=out_specs, check_vma=False
    )
```

```python
import jax
import jax.numpy as jnp
from jax import lax
from jax.sharding import PartitionSpec as P

dual_step = 0.5
primal_step = 0.25
edge_limit = 1.5
AZ_DIGITS = ((8, 2), (2, 4), (1, 2))


def padded_2(block, sides, width):
    for axis, dim in sides:
        count = lax.axis_size(axis)
        forward = [(i, i + 1) for i in range(count - 1)]
        backward = [(target, source) for source, target in forward]
        low = lax.ppermute(
            lax.slice_in_dim(block, block.shape[dim] - width, None, axis=dim), axis, forward
        )
        high = lax.ppermute(lax.slice_in_dim(block, 0, width, axis=dim), axis, backward)
        block = jnp.concatenate([low, block, high], axis=dim)
    return block


def digit_shift(axis, stride, radix, shift):
    count = lax.axis_size(axis)
    pairs = []
    for source in range(count):
        digit = (source // stride) % radix
        pairs.append((source, source + (((digit + shift) % radix) - digit) * stride))
    return pairs


def digits_sum(blocks, axis, digits, stages):
    me = lax.axis_index(axis)
    blocks = blocks.reshape(*[radix for _, radix in digits], *blocks.shape[1:])
    order = [stride for stride, _ in digits]
    for stride, radix in stages:
        place = order.index(stride)
        order.pop(place)
        mine = (me // stride) % radix
        total = lax.dynamic_index_in_dim(blocks, mine, place, keepdims=False)
        for shift in range(1, radix):
            send = lax.dynamic_index_in_dim(blocks, (mine + shift) % radix, place, keepdims=False)
            total = total + lax.ppermute(send, axis, digit_shift(axis, stride, radix, shift))
        blocks = total
    return blocks


def digits_gather(block, axis, stages):
    me = lax.axis_index(axis)
    count = lax.axis_size(axis)
    done = []
    for stride, radix in stages:
        mine = (me // stride) % radix
        got = [block] + [
            lax.ppermute(block, axis, digit_shift(axis, stride, radix, shift))
            for shift in range(1, radix)
        ]
        place = sum(1 for other in done if other > stride)
        source = (mine - jnp.arange(radix, dtype=jnp.int32)) % radix
        block = jnp.take(jnp.stack(got, axis=place), source, axis=place)
        done.append(stride)
    return block.reshape(count, *block.shape[len(stages):])


def on_device(
    image, tv_dual, data_dual, echoes, row_steer, col_steer, kernels, footprint, phase, aperture
):
    highest = lax.Precision.HIGHEST
    az_index = lax.axis_index("az")
    tile_index = lax.axis_index("tile")
    az_count = lax.axis_size("az")
    tile_count = lax.axis_size("tile")
    strip_rows = image.shape[1]
    columns = image.shape[2]
    tiles_dev = row_steer.shape[2]
    tile_rows = row_steer.shape[3]
    rows_dev = data_dual.shape[2]
    range_rows = rows_dev * tile_count
    foot_block = footprint[:, 0, :]
    phase_block = phase[:, 0, :]
    foot_mine = lax.dynamic_slice_in_dim(foot_block, tile_index * tiles_dev, tiles_dev, 0)
    phase_mine = lax.dynamic_slice_in_dim(phase_block, tile_index * tiles_dev, tiles_dev, 0)
    steer_re = row_steer[0]
    steer_im = row_steer[1]
    col_mine = lax.dynamic_slice_in_dim(col_steer, az_index, 1, 3)[..., 0]
    image_b = image.astype(jnp.bfloat16).reshape(2, tiles_dev, tile_rows, columns)
    part_sre = steer_re
    part_sim = steer_im
    weight_re = col_mine[0][..., None]
    weight_im = col_mine[1][..., None]
    prod_re = jnp.einsum("pjh,jhu->pju", part_sre, image_b[0], preferred_element_type=jnp.float32)
    prod_re = prod_re - jnp.einsum(
        "pjh,jhu->pju", part_sim, image_b[1], preferred_element_type=jnp.float32
    )
    prod_im = jnp.einsum("pjh,jhu->pju", part_sre, image_b[1], preferred_element_type=jnp.float32)
    prod_im = prod_im + jnp.einsum(
        "pjh,jhu->pju", part_sim, image_b[0], preferred_element_type=jnp.float32
    )
    real_part = weight_re * prod_re - weight_im * prod_im
    imag_part = weight_re * prod_im + weight_im * prod_re
    parts = jnp.stack([real_part, imag_part], axis=0).reshape(2, az_count, -1, tiles_dev, columns)
    summed = digits_sum(jnp.moveaxis(parts, 1, 0), "az", AZ_DIGITS, ((1, 2), (8, 2), (2, 4)))
    projection_b = jnp.transpose(summed, (2, 1, 0, 3)).astype(jnp.bfloat16)
    all_proj = digits_gather(projection_b, "tile", ((1, 4), (4, 4)))
    all_proj = all_proj.reshape(-1, *all_proj.shape[2:])
    phase_ids = jnp.arange(kernels.shape[0], dtype=jnp.int32)
    my_rows = tile_index * rows_dev + jnp.arange(rows_dev, dtype=jnp.int32)
    hits = (foot_block[:, :, None, None] == my_rows[None, None, :, None]) & (
        phase_block[:, :, None, None] == phase_ids[None, None, None, :]
    )
    counts = jnp.sum(hits.astype(jnp.int32), axis=1).astype(jnp.bfloat16)
    grouped = jnp.einsum(
        "jkq,jpcu->kqpcu", counts, all_proj, preferred_element_type=jnp.float32
    )
    forward = jnp.einsum(
        "kqpcu,quv->cpkv", grouped, kernels.astype(jnp.float32), precision=highest
    )
    kern_mine = kernels[phase_mine]
    live = (aperture == 1)[None, :, None, None]
    dual_new = jnp.where(
        live,
        (data_dual + dual_step * (forward - echoes.astype(jnp.float32))) / (1.0 + dual_step),
        0.0,
    )
    dual_b = dual_new.astype(jnp.bfloat16)
    all_rows = digits_gather(jnp.moveaxis(dual_b, 2, 0), "tile", ((1, 4), (4, 4)))
    all_rows = jnp.moveaxis(all_rows.reshape(-1, *all_rows.shape[2:]), 0, 2)
    chosen = jnp.take(all_rows, foot_mine, axis=2)
    back = jnp.einsum("cpjfv,jfuv->cjpu", chosen, kern_mine, preferred_element_type=jnp.float32)
    back_b = back.astype(jnp.bfloat16)
    piece = digits_gather(jnp.moveaxis(back_b, 2, 0), "az", ((2, 4), (8, 2), (1, 2)))
    piece = jnp.moveaxis(piece.reshape(-1, *piece.shape[2:]), 0, 2)
    weight_re = col_mine[0].T[..., None]
    weight_im = col_mine[1].T[..., None]
    back_re = piece[0].astype(jnp.float32)
    back_im = piece[1].astype(jnp.float32)
    mixed_re = (weight_re * back_re + weight_im * back_im).astype(jnp.bfloat16)
    mixed_im = (weight_re * back_im - weight_im * back_re).astype(jnp.bfloat16)
    part_sre = steer_re
    part_sim = steer_im
    grad_re = jnp.einsum("pjh,jpu->jhu", part_sre, mixed_re, preferred_element_type=jnp.float32)
    grad_re = grad_re + jnp.einsum(
        "pjh,jpu->jhu", part_sim, mixed_im, preferred_element_type=jnp.float32
    )
    grad_im = jnp.einsum("pjh,jpu->jhu", part_sre, mixed_im, preferred_element_type=jnp.float32)
    grad_im = grad_im - jnp.einsum(
        "pjh,jpu->jhu", part_sim, mixed_re, preferred_element_type=jnp.float32
    )
    adjoint = jnp.stack([grad_re, grad_im])
    adjoint = adjoint.reshape(2, strip_rows, columns)
    stacked = jnp.concatenate([image, tv_dual.reshape(4, strip_rows, columns)], axis=0)
    padded = padded_2(stacked, (("az", 2), ("tile", 1)), 1)
    image_pad = padded[:2]
    dual_pad = padded[2:].reshape(2, 2, strip_rows + 2, columns + 2)
    total_rows = tile_count * strip_rows
    total_cols = az_count * columns
    global_row = tile_index * strip_rows - 1 + jnp.arange(strip_rows + 1, dtype=jnp.int32)
    global_col = az_index * columns - 1 + jnp.arange(columns + 1, dtype=jnp.int32)
    centre = image_pad[:, : strip_rows + 1, : columns + 1]
    grad_rows = image_pad[:, 1 : strip_rows + 2, : columns + 1] - centre
    grad_rows = jnp.where((global_row < total_rows - 1)[None, :, None], grad_rows, 0.0)
    grad_cols = image_pad[:, : strip_rows + 1, 1 : columns + 2] - centre
    grad_cols = jnp.where((global_col < total_cols - 1)[None, None, :], grad_cols, 0.0)
    moved = dual_pad[:, :, : strip_rows + 1, : columns + 1] + dual_step * jnp.stack(
        [grad_rows, grad_cols]
    )
    magnitude = jnp.sqrt(jnp.sum(moved * moved, axis=(0, 1)))
    projected = moved / jnp.maximum(1.0, magnitude / edge_limit)
    inside = (global_row >= 0)[:, None] & (global_col >= 0)[None, :]
    projected = jnp.where(inside[None, None], projected, 0.0)
    rows_part = jnp.where((global_row < total_rows - 1)[None, :, None], projected[0], 0.0)
    cols_part = jnp.where((global_col < total_cols - 1)[None, None, :], projected[1], 0.0)
    divergence = (
        rows_part[:, 1:, 1:] - rows_part[:, :-1, 1:] + cols_part[:, 1:, 1:] - cols_part[:, 1:, :-1]
    )
    image_new = image - primal_step * (adjoint - divergence)
    tv_new = projected[:, :, 1:, 1:]
    return (image_new, tv_new, dual_new)


def solution(mesh):
    in_specs = (
        P(None, "tile", "az"),
        P(None, None, "tile", "az"),
        P(None, "az", "tile", None),
        P(None, "az", "tile", None),
        P(None, None, "tile", None),
        P(None, None, "tile", None),
        P(),
        P(None, "az", None),
        P(None, "az", None),
        P("az"),
    )
    out_specs = (P(None, "tile", "az"), P(None, None, "tile", "az"), P(None, "az", "tile", None))
    return jax.shard_map(
        on_device, mesh=mesh, in_specs=in_specs, out_specs=out_specs, check_vma=False
    )
```

```python
import jax
import jax.numpy as jnp
from jax import lax
from jax.sharding import PartitionSpec as P

dual_step = 0.5
primal_step = 0.25
edge_limit = 1.5
AZ_DIGITS = ((8, 2), (2, 4), (1, 2))


def padded_2(block, sides, width):
    for axis, dim in sides:
        count = lax.axis_size(axis)
        forward = [(i, i + 1) for i in range(count - 1)]
        backward = [(target, source) for source, target in forward]
        low = lax.ppermute(
            lax.slice_in_dim(block, block.shape[dim] - width, None, axis=dim), axis, forward
        )
        high = lax.ppermute(lax.slice_in_dim(block, 0, width, axis=dim), axis, backward)
        block = jnp.concatenate([low, block, high], axis=dim)
    return block


def digit_shift(axis, stride, radix, shift):
    count = lax.axis_size(axis)
    pairs = []
    for source in range(count):
        digit = (source // stride) % radix
        pairs.append((source, source + (((digit + shift) % radix) - digit) * stride))
    return pairs


def halves(block):
    half = block.shape[-2] // 2
    return block[..., :half, :], block[..., half:, :]


def stage_sum(blocks, axis, stride, radix, place):
    mine = (lax.axis_index(axis) // stride) % radix

    def pick(offset):
        return lax.dynamic_index_in_dim(blocks, (mine + offset) % radix, place, keepdims=False)

    up = digit_shift(axis, stride, radix, 1)
    if radix == 2:
        return pick(0) + lax.ppermute(pick(1), axis, up)
    down = digit_shift(axis, stride, radix, radix - 1)
    far_low, far_high = halves(pick(2))
    total = pick(0) + lax.ppermute(pick(1), axis, up) + lax.ppermute(pick(3), axis, down)
    relay_low = lax.ppermute(far_low, axis, up)
    relay_high = lax.ppermute(far_high, axis, down)
    far = jnp.concatenate(
        [lax.ppermute(relay_low, axis, up), lax.ppermute(relay_high, axis, down)], axis=-2
    )
    return total + far


def stage_gather(block, axis, stride, radix, place):
    mine = (lax.axis_index(axis) // stride) % radix
    up = digit_shift(axis, stride, radix, 1)
    if radix == 2:
        got = [block, lax.ppermute(block, axis, up)]
    else:
        down = digit_shift(axis, stride, radix, radix - 1)
        from_low = lax.ppermute(block, axis, up)
        from_high = lax.ppermute(block, axis, down)
        far = jnp.concatenate(
            [
                lax.ppermute(halves(from_low)[0], axis, up),
                lax.ppermute(halves(from_high)[1], axis, down),
            ],
            axis=-2,
        )
        got = [block, from_low, far, from_high]
    source = (mine - jnp.arange(radix, dtype=jnp.int32)) % radix
    return jnp.take(jnp.stack(got, axis=place), source, axis=place)


def digits_sum(blocks, axis, digits, stages):
    blocks = blocks.reshape(*[radix for _, radix in digits], *blocks.shape[1:])
    order = [stride for stride, _ in digits]
    for stride, radix in stages:
        place = order.index(stride)
        order.pop(place)
        blocks = stage_sum(blocks, axis, stride, radix, place)
    return blocks


def digits_gather(block, axis, stages):
    count = lax.axis_size(axis)
    done = []
    for stride, radix in stages:
        place = sum(1 for other in done if other > stride)
        block = stage_gather(block, axis, stride, radix, place)
        done.append(stride)
    return block.reshape(count, *block.shape[len(stages):])


def on_device(
    image, tv_dual, data_dual, echoes, row_steer, col_steer, kernels, footprint, phase, aperture
):
    highest = lax.Precision.HIGHEST
    az_index = lax.axis_index("az")
    tile_index = lax.axis_index("tile")
    az_count = lax.axis_size("az")
    tile_count = lax.axis_size("tile")
    strip_rows = image.shape[1]
    columns = image.shape[2]
    tiles_dev = row_steer.shape[2]
    tile_rows = row_steer.shape[3]
    rows_dev = data_dual.shape[2]
    range_rows = rows_dev * tile_count
    foot_block = footprint[:, 0, :]
    phase_block = phase[:, 0, :]
    foot_mine = lax.dynamic_slice_in_dim(foot_block, tile_index * tiles_dev, tiles_dev, 0)
    phase_mine = lax.dynamic_slice_in_dim(phase_block, tile_index * tiles_dev, tiles_dev, 0)
    steer_re = row_steer[0]
    steer_im = row_steer[1]
    col_mine = lax.dynamic_slice_in_dim(col_steer, az_index, 1, 3)[..., 0]
    image_b = image.astype(jnp.bfloat16).reshape(2, tiles_dev, tile_rows, columns)
    part_sre = steer_re
    part_sim = steer_im
    weight_re = col_mine[0][..., None]
    weight_im = col_mine[1][..., None]
    prod_re = jnp.einsum("pjh,jhu->pju", part_sre, image_b[0], preferred_element_type=jnp.float32)
    prod_re = prod_re - jnp.einsum(
        "pjh,jhu->pju", part_sim, image_b[1], preferred_element_type=jnp.float32
    )
    prod_im = jnp.einsum("pjh,jhu->pju", part_sre, image_b[1], preferred_element_type=jnp.float32)
    prod_im = prod_im + jnp.einsum(
        "pjh,jhu->pju", part_sim, image_b[0], preferred_element_type=jnp.float32
    )
    real_part = weight_re * prod_re - weight_im * prod_im
    imag_part = weight_re * prod_im + weight_im * prod_re
    parts = jnp.stack([real_part, imag_part], axis=0).reshape(2, az_count, -1, tiles_dev, columns)
    summed = digits_sum(jnp.moveaxis(parts, 1, 0), "az", AZ_DIGITS, ((1, 2), (2, 4), (8, 2)))
    projection_b = jnp.transpose(summed, (2, 1, 0, 3)).astype(jnp.bfloat16)
    all_proj = digits_gather(projection_b, "tile", ((1, 4), (4, 4)))
    all_proj = all_proj.reshape(-1, *all_proj.shape[2:])
    phase_ids = jnp.arange(kernels.shape[0], dtype=jnp.int32)
    my_rows = tile_index * rows_dev + jnp.arange(rows_dev, dtype=jnp.int32)
    hits = (foot_block[:, :, None, None] == my_rows[None, None, :, None]) & (
        phase_block[:, :, None, None] == phase_ids[None, None, None, :]
    )
    counts = jnp.sum(hits.astype(jnp.int32), axis=1).astype(jnp.bfloat16)
    grouped = jnp.einsum(
        "jkq,jpcu->kqpcu", counts, all_proj, preferred_element_type=jnp.float32
    )
    forward = jnp.einsum(
        "kqpcu,quv->cpkv", grouped, kernels.astype(jnp.float32), precision=highest
    )
    kern_mine = kernels[phase_mine]
    live = (aperture == 1)[None, :, None, None]
    dual_new = jnp.where(
        live,
        (data_dual + dual_step * (forward - echoes.astype(jnp.float32))) / (1.0 + dual_step),
        0.0,
    )
    dual_b = dual_new.astype(jnp.bfloat16)
    all_rows = digits_gather(jnp.moveaxis(dual_b, 2, 0), "tile", ((1, 4), (4, 4)))
    all_rows = jnp.moveaxis(all_rows.reshape(-1, *all_rows.shape[2:]), 0, 2)
    chosen = jnp.take(all_rows, foot_mine, axis=2)
    back = jnp.einsum("cpjfv,jfuv->cjpu", chosen, kern_mine, preferred_element_type=jnp.float32)
    back_b = back.astype(jnp.bfloat16)
    piece = digits_gather(jnp.moveaxis(back_b, 2, 0), "az", ((8, 2), (2, 4), (1, 2)))
    piece = jnp.moveaxis(piece.reshape(-1, *piece.shape[2:]), 0, 2)
    weight_re = col_mine[0].T[..., None]
    weight_im = col_mine[1].T[..., None]
    back_re = piece[0].astype(jnp.float32)
    back_im = piece[1].astype(jnp.float32)
    mixed_re = (weight_re * back_re + weight_im * back_im).astype(jnp.bfloat16)
    mixed_im = (weight_re * back_im - weight_im * back_re).astype(jnp.bfloat16)
    part_sre = steer_re
    part_sim = steer_im
    grad_re = jnp.einsum("pjh,jpu->jhu", part_sre, mixed_re, preferred_element_type=jnp.float32)
    grad_re = grad_re + jnp.einsum(
        "pjh,jpu->jhu", part_sim, mixed_im, preferred_element_type=jnp.float32
    )
    grad_im = jnp.einsum("pjh,jpu->jhu", part_sre, mixed_im, preferred_element_type=jnp.float32)
    grad_im = grad_im - jnp.einsum(
        "pjh,jpu->jhu", part_sim, mixed_re, preferred_element_type=jnp.float32
    )
    adjoint = jnp.stack([grad_re, grad_im])
    adjoint = adjoint.reshape(2, strip_rows, columns)
    stacked = jnp.concatenate([image, tv_dual.reshape(4, strip_rows, columns)], axis=0)
    padded = padded_2(stacked, (("az", 2), ("tile", 1)), 1)
    image_pad = padded[:2]
    dual_pad = padded[2:].reshape(2, 2, strip_rows + 2, columns + 2)
    total_rows = tile_count * strip_rows
    total_cols = az_count * columns
    global_row = tile_index * strip_rows - 1 + jnp.arange(strip_rows + 1, dtype=jnp.int32)
    global_col = az_index * columns - 1 + jnp.arange(columns + 1, dtype=jnp.int32)
    centre = image_pad[:, : strip_rows + 1, : columns + 1]
    grad_rows = image_pad[:, 1 : strip_rows + 2, : columns + 1] - centre
    grad_rows = jnp.where((global_row < total_rows - 1)[None, :, None], grad_rows, 0.0)
    grad_cols = image_pad[:, : strip_rows + 1, 1 : columns + 2] - centre
    grad_cols = jnp.where((global_col < total_cols - 1)[None, None, :], grad_cols, 0.0)
    moved = dual_pad[:, :, : strip_rows + 1, : columns + 1] + dual_step * jnp.stack(
        [grad_rows, grad_cols]
    )
    magnitude = jnp.sqrt(jnp.sum(moved * moved, axis=(0, 1)))
    projected = moved / jnp.maximum(1.0, magnitude / edge_limit)
    inside = (global_row >= 0)[:, None] & (global_col >= 0)[None, :]
    projected = jnp.where(inside[None, None], projected, 0.0)
    rows_part = jnp.where((global_row < total_rows - 1)[None, :, None], projected[0], 0.0)
    cols_part = jnp.where((global_col < total_cols - 1)[None, None, :], projected[1], 0.0)
    divergence = (
        rows_part[:, 1:, 1:] - rows_part[:, :-1, 1:] + cols_part[:, 1:, 1:] - cols_part[:, 1:, :-1]
    )
    image_new = image - primal_step * (adjoint - divergence)
    tv_new = projected[:, :, 1:, 1:]
    return (image_new, tv_new, dual_new)


def solution(mesh):
    in_specs = (
        P(None, "tile", "az"),
        P(None, None, "tile", "az"),
        P(None, "az", "tile", None),
        P(None, "az", "tile", None),
        P(None, None, "tile", None),
        P(None, None, "tile", None),
        P(),
        P(None, "az", None),
        P(None, "az", None),
        P("az"),
    )
    out_specs = (P(None, "tile", "az"), P(None, None, "tile", "az"), P(None, "az", "tile", None))
    return jax.shard_map(
        on_device, mesh=mesh, in_specs=in_specs, out_specs=out_specs, check_vma=False
    )
```

```python
import jax
import jax.numpy as jnp
from jax import lax
from jax.sharding import PartitionSpec as P

dual_step = 0.5
primal_step = 0.25
edge_limit = 1.5


def padded_2(block, sides, width):
    for axis, dim in sides:
        count = lax.axis_size(axis)
        forward = [(i, i + 1) for i in range(count - 1)]
        backward = [(target, source) for source, target in forward]
        low = lax.ppermute(
            lax.slice_in_dim(block, block.shape[dim] - width, None, axis=dim), axis, forward
        )
        high = lax.ppermute(lax.slice_in_dim(block, 0, width, axis=dim), axis, backward)
        block = jnp.concatenate([low, block, high], axis=dim)
    return block


def halving_sum(blocks, axis, bits):
    me = lax.axis_index(axis)
    count = lax.axis_size(axis)
    order = [count >> (level + 1) for level in range(count.bit_length() - 1)]
    blocks = blocks.reshape(*([2] * len(order)), *blocks.shape[1:])
    for bit in bits:
        place = order.index(bit)
        order.pop(place)
        mine = (me // bit) % 2
        keep = lax.dynamic_index_in_dim(blocks, mine, place, keepdims=False)
        send = lax.dynamic_index_in_dim(blocks, 1 - mine, place, keepdims=False)
        pairs = [(i, i ^ bit) for i in range(count)]
        blocks = keep + lax.ppermute(send, axis, pairs)
    return blocks


def doubling_gather(block, axis, bits):
    me = lax.axis_index(axis)
    count = lax.axis_size(axis)
    done = []
    for bit in bits:
        mine = (me // bit) % 2
        pairs = [(i, i ^ bit) for i in range(count)]
        got = lax.ppermute(block, axis, pairs)
        place = sum(1 for other in done if other > bit)
        low = jnp.where(mine == 0, block, got)
        high = jnp.where(mine == 0, got, block)
        block = jnp.stack([low, high], axis=place)
        done.append(bit)
    return block.reshape(count, *block.shape[len(bits):])


def on_device(
    image, tv_dual, data_dual, echoes, row_steer, col_steer, kernels, footprint, phase, aperture
):
    highest = lax.Precision.HIGHEST
    az_index = lax.axis_index("az")
    tile_index = lax.axis_index("tile")
    az_count = lax.axis_size("az")
    tile_count = lax.axis_size("tile")
    strip_rows = image.shape[1]
    columns = image.shape[2]
    tiles_dev = row_steer.shape[2]
    tile_rows = row_steer.shape[3]
    rows_dev = data_dual.shape[2]
    range_rows = rows_dev * tile_count
    foot_block = footprint[:, 0, :]
    phase_block = phase[:, 0, :]
    foot_mine = lax.dynamic_slice_in_dim(foot_block, tile_index * tiles_dev, tiles_dev, 0)
    phase_mine = lax.dynamic_slice_in_dim(phase_block, tile_index * tiles_dev, tiles_dev, 0)
    steer_re = row_steer[0]
    steer_im = row_steer[1]
    col_mine = lax.dynamic_slice_in_dim(col_steer, az_index, 1, 3)[..., 0]
    image_b = image.astype(jnp.bfloat16).reshape(2, tiles_dev, tile_rows, columns)
    part_sre = steer_re
    part_sim = steer_im
    weight_re = col_mine[0][..., None]
    weight_im = col_mine[1][..., None]
    prod_re = jnp.einsum("pjh,jhu->pju", part_sre, image_b[0], preferred_element_type=jnp.float32)
    prod_re = prod_re - jnp.einsum(
        "pjh,jhu->pju", part_sim, image_b[1], preferred_element_type=jnp.float32
    )
    prod_im = jnp.einsum("pjh,jhu->pju", part_sre, image_b[1], preferred_element_type=jnp.float32)
    prod_im = prod_im + jnp.einsum(
        "pjh,jhu->pju", part_sim, image_b[0], preferred_element_type=jnp.float32
    )
    real_part = weight_re * prod_re - weight_im * prod_im
    imag_part = weight_re * prod_im + weight_im * prod_re
    parts = jnp.stack([real_part, imag_part], axis=0).reshape(2, az_count, -1, tiles_dev, columns)
    summed = halving_sum(jnp.moveaxis(parts, 1, 0), "az", (1, 8, 2, 4))
    projection_b = jnp.transpose(summed, (2, 1, 0, 3)).astype(jnp.bfloat16)
    all_proj = doubling_gather(projection_b, "tile", (2, 1, 8, 4))
    all_proj = all_proj.reshape(-1, *all_proj.shape[2:])
    phase_ids = jnp.arange(kernels.shape[0], dtype=jnp.int32)
    my_rows = tile_index * rows_dev + jnp.arange(rows_dev, dtype=jnp.int32)
    hits = (foot_block[:, :, None, None] == my_rows[None, None, :, None]) & (
        phase_block[:, :, None, None] == phase_ids[None, None, None, :]
    )
    counts = jnp.sum(hits.astype(jnp.int32), axis=1).astype(jnp.bfloat16)
    grouped = jnp.einsum(
        "jkq,jpcu->kqpcu", counts, all_proj, preferred_element_type=jnp.float32
    )
    forward = jnp.einsum(
        "kqpcu,quv->cpkv", grouped, kernels.astype(jnp.float32), precision=highest
    )
    kern_mine = kernels[phase_mine]
    live = (aperture == 1)[None, :, None, None]
    dual_new = jnp.where(
        live,
        (data_dual + dual_step * (forward - echoes.astype(jnp.float32))) / (1.0 + dual_step),
        0.0,
    )
    dual_b = dual_new.astype(jnp.bfloat16)
    all_rows = lax.all_gather(dual_b, "tile", axis=2, tiled=True)
    chosen = jnp.take(all_rows, foot_mine, axis=2)
    back = jnp.einsum("cpjfv,jfuv->cjpu", chosen, kern_mine, preferred_element_type=jnp.float32)
    back_b = back.astype(jnp.bfloat16)
    piece = doubling_gather(jnp.moveaxis(back_b, 2, 0), "az", (4, 8, 2, 1))
    piece = jnp.moveaxis(piece.reshape(-1, *piece.shape[2:]), 0, 2)
    weight_re = col_mine[0].T[..., None]
    weight_im = col_mine[1].T[..., None]
    back_re = piece[0].astype(jnp.float32)
    back_im = piece[1].astype(jnp.float32)
    mixed_re = (weight_re * back_re + weight_im * back_im).astype(jnp.bfloat16)
    mixed_im = (weight_re * back_im - weight_im * back_re).astype(jnp.bfloat16)
    part_sre = steer_re
    part_sim = steer_im
    grad_re = jnp.einsum("pjh,jpu->jhu", part_sre, mixed_re, preferred_element_type=jnp.float32)
    grad_re = grad_re + jnp.einsum(
        "pjh,jpu->jhu", part_sim, mixed_im, preferred_element_type=jnp.float32
    )
    grad_im = jnp.einsum("pjh,jpu->jhu", part_sre, mixed_im, preferred_element_type=jnp.float32)
    grad_im = grad_im - jnp.einsum(
        "pjh,jpu->jhu", part_sim, mixed_re, preferred_element_type=jnp.float32
    )
    adjoint = jnp.stack([grad_re, grad_im])
    adjoint = adjoint.reshape(2, strip_rows, columns)
    stacked = jnp.concatenate([image, tv_dual.reshape(4, strip_rows, columns)], axis=0)
    padded = padded_2(stacked, (("az", 2), ("tile", 1)), 1)
    image_pad = padded[:2]
    dual_pad = padded[2:].reshape(2, 2, strip_rows + 2, columns + 2)
    total_rows = tile_count * strip_rows
    total_cols = az_count * columns
    global_row = tile_index * strip_rows - 1 + jnp.arange(strip_rows + 1, dtype=jnp.int32)
    global_col = az_index * columns - 1 + jnp.arange(columns + 1, dtype=jnp.int32)
    centre = image_pad[:, : strip_rows + 1, : columns + 1]
    grad_rows = image_pad[:, 1 : strip_rows + 2, : columns + 1] - centre
    grad_rows = jnp.where((global_row < total_rows - 1)[None, :, None], grad_rows, 0.0)
    grad_cols = image_pad[:, : strip_rows + 1, 1 : columns + 2] - centre
    grad_cols = jnp.where((global_col < total_cols - 1)[None, None, :], grad_cols, 0.0)
    moved = dual_pad[:, :, : strip_rows + 1, : columns + 1] + dual_step * jnp.stack(
        [grad_rows, grad_cols]
    )
    magnitude = jnp.sqrt(jnp.sum(moved * moved, axis=(0, 1)))
    projected = moved / jnp.maximum(1.0, magnitude / edge_limit)
    inside = (global_row >= 0)[:, None] & (global_col >= 0)[None, :]
    projected = jnp.where(inside[None, None], projected, 0.0)
    rows_part = jnp.where((global_row < total_rows - 1)[None, :, None], projected[0], 0.0)
    cols_part = jnp.where((global_col < total_cols - 1)[None, None, :], projected[1], 0.0)
    divergence = (
        rows_part[:, 1:, 1:] - rows_part[:, :-1, 1:] + cols_part[:, 1:, 1:] - cols_part[:, 1:, :-1]
    )
    image_new = image - primal_step * (adjoint - divergence)
    tv_new = projected[:, :, 1:, 1:]
    return (image_new, tv_new, dual_new)


def solution(mesh):
    in_specs = (
        P(None, "tile", "az"),
        P(None, None, "tile", "az"),
        P(None, "az", "tile", None),
        P(None, "az", "tile", None),
        P(None, None, "tile", None),
        P(None, None, "tile", None),
        P(),
        P(None, "az", None),
        P(None, "az", None),
        P("az"),
    )
    out_specs = (P(None, "tile", "az"), P(None, None, "tile", "az"), P(None, "az", "tile", None))
    return jax.shard_map(
        on_device, mesh=mesh, in_specs=in_specs, out_specs=out_specs, check_vma=False
    )
```

```python
import jax
import jax.numpy as jnp
from jax import lax
from jax.sharding import PartitionSpec as P

dual_step = 0.5
primal_step = 0.25
edge_limit = 1.5


def padded_2(block, sides, width):
    for axis, dim in sides:
        count = lax.axis_size(axis)
        forward = [(i, i + 1) for i in range(count - 1)]
        backward = [(target, source) for source, target in forward]
        low = lax.ppermute(
            lax.slice_in_dim(block, block.shape[dim] - width, None, axis=dim), axis, forward
        )
        high = lax.ppermute(lax.slice_in_dim(block, 0, width, axis=dim), axis, backward)
        block = jnp.concatenate([low, block, high], axis=dim)
    return block


def halving_sum(blocks, axis, bits):
    me = lax.axis_index(axis)
    count = lax.axis_size(axis)
    order = [count >> (level + 1) for level in range(count.bit_length() - 1)]
    blocks = blocks.reshape(*([2] * len(order)), *blocks.shape[1:])
    for bit in bits:
        place = order.index(bit)
        order.pop(place)
        mine = (me // bit) % 2
        keep = lax.dynamic_index_in_dim(blocks, mine, place, keepdims=False)
        send = lax.dynamic_index_in_dim(blocks, 1 - mine, place, keepdims=False)
        pairs = [(i, i ^ bit) for i in range(count)]
        blocks = keep + lax.ppermute(send, axis, pairs)
    return blocks


def doubling_gather(block, axis, bits):
    me = lax.axis_index(axis)
    count = lax.axis_size(axis)
    done = []
    for bit in bits:
        mine = (me // bit) % 2
        pairs = [(i, i ^ bit) for i in range(count)]
        got = lax.ppermute(block, axis, pairs)
        place = sum(1 for other in done if other > bit)
        low = jnp.where(mine == 0, block, got)
        high = jnp.where(mine == 0, got, block)
        block = jnp.stack([low, high], axis=place)
        done.append(bit)
    return block.reshape(count, *block.shape[len(bits):])


def on_device(
    image, tv_dual, data_dual, echoes, row_steer, col_steer, kernels, footprint, phase, aperture
):
    highest = lax.Precision.HIGHEST
    az_index = lax.axis_index("az")
    tile_index = lax.axis_index("tile")
    az_count = lax.axis_size("az")
    tile_count = lax.axis_size("tile")
    strip_rows = image.shape[1]
    columns = image.shape[2]
    tiles_dev = row_steer.shape[2]
    tile_rows = row_steer.shape[3]
    rows_dev = data_dual.shape[2]
    range_rows = rows_dev * tile_count
    foot_block = footprint[:, 0, :]
    phase_block = phase[:, 0, :]
    foot_mine = lax.dynamic_slice_in_dim(foot_block, tile_index * tiles_dev, tiles_dev, 0)
    phase_mine = lax.dynamic_slice_in_dim(phase_block, tile_index * tiles_dev, tiles_dev, 0)
    steer_re = row_steer[0]
    steer_im = row_steer[1]
    col_mine = lax.dynamic_slice_in_dim(col_steer, az_index, 1, 3)[..., 0]
    image_b = image.astype(jnp.bfloat16).reshape(2, tiles_dev, tile_rows, columns)
    part_sre = steer_re
    part_sim = steer_im
    weight_re = col_mine[0][..., None]
    weight_im = col_mine[1][..., None]
    prod_re = jnp.einsum("pjh,jhu->pju", part_sre, image_b[0], preferred_element_type=jnp.float32)
    prod_re = prod_re - jnp.einsum(
        "pjh,jhu->pju", part_sim, image_b[1], preferred_element_type=jnp.float32
    )
    prod_im = jnp.einsum("pjh,jhu->pju", part_sre, image_b[1], preferred_element_type=jnp.float32)
    prod_im = prod_im + jnp.einsum(
        "pjh,jhu->pju", part_sim, image_b[0], preferred_element_type=jnp.float32
    )
    real_part = weight_re * prod_re - weight_im * prod_im
    imag_part = weight_re * prod_im + weight_im * prod_re
    parts = jnp.stack([real_part, imag_part], axis=0).reshape(2, az_count, -1, tiles_dev, columns)
    summed = halving_sum(jnp.moveaxis(parts, 1, 0), "az", (1, 8, 2, 4))
    projection_b = jnp.transpose(summed, (2, 1, 0, 3)).astype(jnp.bfloat16)
    stacked = jnp.concatenate([image, tv_dual.reshape(4, strip_rows, columns)], axis=0)
    padded = padded_2(stacked, (("az", 2), ("tile", 1)), 1)
    padded, projection_b = lax.optimization_barrier((padded, projection_b))
    all_proj = doubling_gather(projection_b, "tile", (2, 1, 8, 4))
    all_proj = all_proj.reshape(-1, *all_proj.shape[2:])
    phase_ids = jnp.arange(kernels.shape[0], dtype=jnp.int32)
    my_rows = tile_index * rows_dev + jnp.arange(rows_dev, dtype=jnp.int32)
    hits = (foot_block[:, :, None, None] == my_rows[None, None, :, None]) & (
        phase_block[:, :, None, None] == phase_ids[None, None, None, :]
    )
    counts = jnp.sum(hits.astype(jnp.int32), axis=1).astype(jnp.bfloat16)
    grouped = jnp.einsum(
        "jkq,jpcu->kqpcu", counts, all_proj, preferred_element_type=jnp.float32
    )
    forward = jnp.einsum(
        "kqpcu,quv->cpkv", grouped, kernels.astype(jnp.float32), precision=highest
    )
    kern_mine = kernels[phase_mine]
    live = (aperture == 1)[None, :, None, None]
    dual_new = jnp.where(
        live,
        (data_dual + dual_step * (forward - echoes.astype(jnp.float32))) / (1.0 + dual_step),
        0.0,
    )
    dual_b = dual_new.astype(jnp.bfloat16)
    all_rows = doubling_gather(jnp.moveaxis(dual_b, 2, 0), "tile", (2, 1, 8, 4))
    all_rows = jnp.moveaxis(all_rows.reshape(-1, *all_rows.shape[2:]), 0, 2)
    chosen = jnp.take(all_rows, foot_mine, axis=2)
    back = jnp.einsum("cpjfv,jfuv->cjpu", chosen, kern_mine, preferred_element_type=jnp.float32)
    back_b = back.astype(jnp.bfloat16)
    piece = doubling_gather(jnp.moveaxis(back_b, 2, 0), "az", (4, 8, 2, 1))
    piece = jnp.moveaxis(piece.reshape(-1, *piece.shape[2:]), 0, 2)
    weight_re = col_mine[0].T[..., None]
    weight_im = col_mine[1].T[..., None]
    back_re = piece[0].astype(jnp.float32)
    back_im = piece[1].astype(jnp.float32)
    mixed_re = (weight_re * back_re + weight_im * back_im).astype(jnp.bfloat16)
    mixed_im = (weight_re * back_im - weight_im * back_re).astype(jnp.bfloat16)
    part_sre = steer_re
    part_sim = steer_im
    grad_re = jnp.einsum("pjh,jpu->jhu", part_sre, mixed_re, preferred_element_type=jnp.float32)
    grad_re = grad_re + jnp.einsum(
        "pjh,jpu->jhu", part_sim, mixed_im, preferred_element_type=jnp.float32
    )
    grad_im = jnp.einsum("pjh,jpu->jhu", part_sre, mixed_im, preferred_element_type=jnp.float32)
    grad_im = grad_im - jnp.einsum(
        "pjh,jpu->jhu", part_sim, mixed_re, preferred_element_type=jnp.float32
    )
    adjoint = jnp.stack([grad_re, grad_im])
    adjoint = adjoint.reshape(2, strip_rows, columns)
    image_pad = padded[:2]
    dual_pad = padded[2:].reshape(2, 2, strip_rows + 2, columns + 2)
    total_rows = tile_count * strip_rows
    total_cols = az_count * columns
    global_row = tile_index * strip_rows - 1 + jnp.arange(strip_rows + 1, dtype=jnp.int32)
    global_col = az_index * columns - 1 + jnp.arange(columns + 1, dtype=jnp.int32)
    centre = image_pad[:, : strip_rows + 1, : columns + 1]
    grad_rows = image_pad[:, 1 : strip_rows + 2, : columns + 1] - centre
    grad_rows = jnp.where((global_row < total_rows - 1)[None, :, None], grad_rows, 0.0)
    grad_cols = image_pad[:, : strip_rows + 1, 1 : columns + 2] - centre
    grad_cols = jnp.where((global_col < total_cols - 1)[None, None, :], grad_cols, 0.0)
    moved = dual_pad[:, :, : strip_rows + 1, : columns + 1] + dual_step * jnp.stack(
        [grad_rows, grad_cols]
    )
    magnitude = jnp.sqrt(jnp.sum(moved * moved, axis=(0, 1)))
    projected = moved / jnp.maximum(1.0, magnitude / edge_limit)
    inside = (global_row >= 0)[:, None] & (global_col >= 0)[None, :]
    projected = jnp.where(inside[None, None], projected, 0.0)
    rows_part = jnp.where((global_row < total_rows - 1)[None, :, None], projected[0], 0.0)
    cols_part = jnp.where((global_col < total_cols - 1)[None, None, :], projected[1], 0.0)
    divergence = (
        rows_part[:, 1:, 1:] - rows_part[:, :-1, 1:] + cols_part[:, 1:, 1:] - cols_part[:, 1:, :-1]
    )
    image_new = image - primal_step * (adjoint - divergence)
    tv_new = projected[:, :, 1:, 1:]
    return (image_new, tv_new, dual_new)


def solution(mesh):
    in_specs = (
        P(None, "tile", "az"),
        P(None, None, "tile", "az"),
        P(None, "az", "tile", None),
        P(None, "az", "tile", None),
        P(None, None, "tile", None),
        P(None, None, "tile", None),
        P(),
        P(None, "az", None),
        P(None, "az", None),
        P("az"),
    )
    out_specs = (P(None, "tile", "az"), P(None, None, "tile", "az"), P(None, "az", "tile", None))
    return jax.shard_map(
        on_device, mesh=mesh, in_specs=in_specs, out_specs=out_specs, check_vma=False
    )
```

```python
import jax
import jax.numpy as jnp
from jax import lax
from jax.sharding import PartitionSpec as P

dual_step = 0.5
primal_step = 0.25
edge_limit = 1.5
AZ_DIGITS = ((8, 2), (4, 2), (2, 2), (1, 2))


def padded_2(block, sides, width):
    for axis, dim in sides:
        count = lax.axis_size(axis)
        forward = [(i, i + 1) for i in range(count - 1)]
        backward = [(target, source) for source, target in forward]
        low = lax.ppermute(
            lax.slice_in_dim(block, block.shape[dim] - width, None, axis=dim), axis, forward
        )
        high = lax.ppermute(lax.slice_in_dim(block, 0, width, axis=dim), axis, backward)
        block = jnp.concatenate([low, block, high], axis=dim)
    return block


def digit_shift(axis, stride, radix, shift):
    count = lax.axis_size(axis)
    pairs = []
    for source in range(count):
        digit = (source // stride) % radix
        pairs.append((source, source + (((digit + shift) % radix) - digit) * stride))
    return pairs


def halves(block):
    half = block.shape[-2] // 2
    return block[..., :half, :], block[..., half:, :]


def stage_sum(blocks, axis, stride, radix, place):
    mine = (lax.axis_index(axis) // stride) % radix

    def pick(offset):
        return lax.dynamic_index_in_dim(blocks, (mine + offset) % radix, place, keepdims=False)

    up = digit_shift(axis, stride, radix, 1)
    if radix == 2:
        return pick(0) + lax.ppermute(pick(1), axis, up)
    down = digit_shift(axis, stride, radix, radix - 1)
    far_low, far_high = halves(pick(2))
    total = pick(0) + lax.ppermute(pick(1), axis, up) + lax.ppermute(pick(3), axis, down)
    relay_low = lax.ppermute(far_low, axis, up)
    relay_high = lax.ppermute(far_high, axis, down)
    far = jnp.concatenate(
        [lax.ppermute(relay_low, axis, up), lax.ppermute(relay_high, axis, down)], axis=-2
    )
    return total + far


def stage_gather(block, axis, stride, radix, place):
    mine = (lax.axis_index(axis) // stride) % radix
    up = digit_shift(axis, stride, radix, 1)
    if radix == 2:
        got = [block, lax.ppermute(block, axis, up)]
    else:
        down = digit_shift(axis, stride, radix, radix - 1)
        from_low = lax.ppermute(block, axis, up)
        from_high = lax.ppermute(block, axis, down)
        far = jnp.concatenate(
            [
                lax.ppermute(halves(from_low)[0], axis, up),
                lax.ppermute(halves(from_high)[1], axis, down),
            ],
            axis=-2,
        )
        got = [block, from_low, far, from_high]
    source = (mine - jnp.arange(radix, dtype=jnp.int32)) % radix
    return jnp.take(jnp.stack(got, axis=place), source, axis=place)


def digits_sum(blocks, axis, digits, stages):
    blocks = blocks.reshape(*[radix for _, radix in digits], *blocks.shape[1:])
    order = [stride for stride, _ in digits]
    for stride, radix in stages:
        place = order.index(stride)
        order.pop(place)
        blocks = stage_sum(blocks, axis, stride, radix, place)
    return blocks


def digits_gather(block, axis, stages):
    count = lax.axis_size(axis)
    done = []
    for stride, radix in stages:
        place = sum(1 for other in done if other > stride)
        block = stage_gather(block, axis, stride, radix, place)
        done.append(stride)
    return block.reshape(count, *block.shape[len(stages):])


def on_device(
    image, tv_dual, data_dual, echoes, row_steer, col_steer, kernels, footprint, phase, aperture
):
    highest = lax.Precision.HIGHEST
    az_index = lax.axis_index("az")
    tile_index = lax.axis_index("tile")
    az_count = lax.axis_size("az")
    tile_count = lax.axis_size("tile")
    strip_rows = image.shape[1]
    columns = image.shape[2]
    tiles_dev = row_steer.shape[2]
    tile_rows = row_steer.shape[3]
    rows_dev = data_dual.shape[2]
    range_rows = rows_dev * tile_count
    foot_block = footprint[:, 0, :]
    phase_block = phase[:, 0, :]
    foot_mine = lax.dynamic_slice_in_dim(foot_block, tile_index * tiles_dev, tiles_dev, 0)
    phase_mine = lax.dynamic_slice_in_dim(phase_block, tile_index * tiles_dev, tiles_dev, 0)
    steer_re = row_steer[0]
    steer_im = row_steer[1]
    col_mine = lax.dynamic_slice_in_dim(col_steer, az_index, 1, 3)[..., 0]
    image_b = image.astype(jnp.bfloat16).reshape(2, tiles_dev, tile_rows, columns)
    part_sre = steer_re
    part_sim = steer_im
    weight_re = col_mine[0][..., None]
    weight_im = col_mine[1][..., None]
    prod_re = jnp.einsum("pjh,jhu->pju", part_sre, image_b[0], preferred_element_type=jnp.float32)
    prod_re = prod_re - jnp.einsum(
        "pjh,jhu->pju", part_sim, image_b[1], preferred_element_type=jnp.float32
    )
    prod_im = jnp.einsum("pjh,jhu->pju", part_sre, image_b[1], preferred_element_type=jnp.float32)
    prod_im = prod_im + jnp.einsum(
        "pjh,jhu->pju", part_sim, image_b[0], preferred_element_type=jnp.float32
    )
    real_part = weight_re * prod_re - weight_im * prod_im
    imag_part = weight_re * prod_im + weight_im * prod_re
    parts = jnp.stack([real_part, imag_part], axis=0).reshape(2, az_count, -1, tiles_dev, columns)
    summed = digits_sum(jnp.moveaxis(parts, 1, 0), "az", AZ_DIGITS, ((1, 2), (8, 2), (2, 2), (4, 2)))
    projection_b = jnp.transpose(summed, (2, 1, 0, 3)).astype(jnp.bfloat16)
    all_proj = digits_gather(projection_b, "tile", ((2, 2), (1, 2), (8, 2), (4, 2)))
    all_proj = all_proj.reshape(-1, *all_proj.shape[2:])
    phase_ids = jnp.arange(kernels.shape[0], dtype=jnp.int32)
    my_rows = tile_index * rows_dev + jnp.arange(rows_dev, dtype=jnp.int32)
    hits = (foot_block[:, :, None, None] == my_rows[None, None, :, None]) & (
        phase_block[:, :, None, None] == phase_ids[None, None, None, :]
    )
    counts = jnp.sum(hits.astype(jnp.int32), axis=1).astype(jnp.bfloat16)
    grouped = jnp.einsum(
        "jkq,jpcu->kqpcu", counts, all_proj, preferred_element_type=jnp.float32
    )
    forward = jnp.einsum(
        "kqpcu,quv->cpkv", grouped, kernels.astype(jnp.float32), precision=highest
    )
    kern_mine = kernels[phase_mine]
    live = (aperture == 1)[None, :, None, None]
    dual_new = jnp.where(
        live,
        (data_dual + dual_step * (forward - echoes.astype(jnp.float32))) / (1.0 + dual_step),
        0.0,
    )
    dual_b = dual_new.astype(jnp.bfloat16)
    all_rows = digits_gather(jnp.moveaxis(dual_b, 2, 0), "tile", ((2, 2), (1, 2), (4, 4)))
    all_rows = jnp.moveaxis(all_rows.reshape(-1, *all_rows.shape[2:]), 0, 2)
    chosen = jnp.take(all_rows, foot_mine, axis=2)
    back = jnp.einsum("cpjfv,jfuv->cjpu", chosen, kern_mine, preferred_element_type=jnp.float32)
    back_b = back.astype(jnp.bfloat16)
    piece = digits_gather(jnp.moveaxis(back_b, 2, 0), "az", ((4, 2), (8, 2), (2, 2), (1, 2)))
    piece = jnp.moveaxis(piece.reshape(-1, *piece.shape[2:]), 0, 2)
    weight_re = col_mine[0].T[..., None]
    weight_im = col_mine[1].T[..., None]
    back_re = piece[0].astype(jnp.float32)
    back_im = piece[1].astype(jnp.float32)
    mixed_re = (weight_re * back_re + weight_im * back_im).astype(jnp.bfloat16)
    mixed_im = (weight_re * back_im - weight_im * back_re).astype(jnp.bfloat16)
    part_sre = steer_re
    part_sim = steer_im
    grad_re = jnp.einsum("pjh,jpu->jhu", part_sre, mixed_re, preferred_element_type=jnp.float32)
    grad_re = grad_re + jnp.einsum(
        "pjh,jpu->jhu", part_sim, mixed_im, preferred_element_type=jnp.float32
    )
    grad_im = jnp.einsum("pjh,jpu->jhu", part_sre, mixed_im, preferred_element_type=jnp.float32)
    grad_im = grad_im - jnp.einsum(
        "pjh,jpu->jhu", part_sim, mixed_re, preferred_element_type=jnp.float32
    )
    adjoint = jnp.stack([grad_re, grad_im])
    adjoint = adjoint.reshape(2, strip_rows, columns)
    stacked = jnp.concatenate([image, tv_dual.reshape(4, strip_rows, columns)], axis=0)
    padded = padded_2(stacked, (("az", 2), ("tile", 1)), 1)
    image_pad = padded[:2]
    dual_pad = padded[2:].reshape(2, 2, strip_rows + 2, columns + 2)
    total_rows = tile_count * strip_rows
    total_cols = az_count * columns
    global_row = tile_index * strip_rows - 1 + jnp.arange(strip_rows + 1, dtype=jnp.int32)
    global_col = az_index * columns - 1 + jnp.arange(columns + 1, dtype=jnp.int32)
    centre = image_pad[:, : strip_rows + 1, : columns + 1]
    grad_rows = image_pad[:, 1 : strip_rows + 2, : columns + 1] - centre
    grad_rows = jnp.where((global_row < total_rows - 1)[None, :, None], grad_rows, 0.0)
    grad_cols = image_pad[:, : strip_rows + 1, 1 : columns + 2] - centre
    grad_cols = jnp.where((global_col < total_cols - 1)[None, None, :], grad_cols, 0.0)
    moved = dual_pad[:, :, : strip_rows + 1, : columns + 1] + dual_step * jnp.stack(
        [grad_rows, grad_cols]
    )
    magnitude = jnp.sqrt(jnp.sum(moved * moved, axis=(0, 1)))
    projected = moved / jnp.maximum(1.0, magnitude / edge_limit)
    inside = (global_row >= 0)[:, None] & (global_col >= 0)[None, :]
    projected = jnp.where(inside[None, None], projected, 0.0)
    rows_part = jnp.where((global_row < total_rows - 1)[None, :, None], projected[0], 0.0)
    cols_part = jnp.where((global_col < total_cols - 1)[None, None, :], projected[1], 0.0)
    divergence = (
        rows_part[:, 1:, 1:] - rows_part[:, :-1, 1:] + cols_part[:, 1:, 1:] - cols_part[:, 1:, :-1]
    )
    image_new = image - primal_step * (adjoint - divergence)
    tv_new = projected[:, :, 1:, 1:]
    return (image_new, tv_new, dual_new)


def solution(mesh):
    in_specs = (
        P(None, "tile", "az"),
        P(None, None, "tile", "az"),
        P(None, "az", "tile", None),
        P(None, "az", "tile", None),
        P(None, None, "tile", None),
        P(None, None, "tile", None),
        P(),
        P(None, "az", None),
        P(None, "az", None),
        P("az"),
    )
    out_specs = (P(None, "tile", "az"), P(None, None, "tile", "az"), P(None, "az", "tile", None))
    return jax.shard_map(
        on_device, mesh=mesh, in_specs=in_specs, out_specs=out_specs, check_vma=False
    )
```

```python
import jax
import jax.numpy as jnp
from jax import lax
from jax.sharding import PartitionSpec as P

dual_step = 0.5
primal_step = 0.25
edge_limit = 1.5


def padded_2(block, sides, width):
    for axis, dim in sides:
        count = lax.axis_size(axis)
        forward = [(i, i + 1) for i in range(count - 1)]
        backward = [(target, source) for source, target in forward]
        low = lax.ppermute(
            lax.slice_in_dim(block, block.shape[dim] - width, None, axis=dim), axis, forward
        )
        high = lax.ppermute(lax.slice_in_dim(block, 0, width, axis=dim), axis, backward)
        block = jnp.concatenate([low, block, high], axis=dim)
    return block


def halving_sum(blocks, axis, bits):
    me = lax.axis_index(axis)
    count = lax.axis_size(axis)
    order = [count >> (level + 1) for level in range(count.bit_length() - 1)]
    blocks = blocks.reshape(*([2] * len(order)), *blocks.shape[1:])
    for bit in bits:
        place = order.index(bit)
        order.pop(place)
        mine = (me // bit) % 2
        keep = lax.dynamic_index_in_dim(blocks, mine, place, keepdims=False)
        send = lax.dynamic_index_in_dim(blocks, 1 - mine, place, keepdims=False)
        pairs = [(i, i ^ bit) for i in range(count)]
        blocks = keep + lax.ppermute(send, axis, pairs)
    return blocks


def doubling_gather(block, axis, bits):
    me = lax.axis_index(axis)
    count = lax.axis_size(axis)
    done = []
    for bit in bits:
        mine = (me // bit) % 2
        pairs = [(i, i ^ bit) for i in range(count)]
        got = lax.ppermute(block, axis, pairs)
        place = sum(1 for other in done if other > bit)
        low = jnp.where(mine == 0, block, got)
        high = jnp.where(mine == 0, got, block)
        block = jnp.stack([low, high], axis=place)
        done.append(bit)
    return block.reshape(count, *block.shape[len(bits):])


def on_device(
    image, tv_dual, data_dual, echoes, row_steer, col_steer, kernels, footprint, phase, aperture
):
    highest = lax.Precision.HIGHEST
    az_index = lax.axis_index("az")
    tile_index = lax.axis_index("tile")
    az_count = lax.axis_size("az")
    tile_count = lax.axis_size("tile")
    strip_rows = image.shape[1]
    columns = image.shape[2]
    tiles_dev = row_steer.shape[2]
    tile_rows = row_steer.shape[3]
    rows_dev = data_dual.shape[2]
    range_rows = rows_dev * tile_count
    foot_block = footprint[:, 0, :]
    phase_block = phase[:, 0, :]
    foot_mine = lax.dynamic_slice_in_dim(foot_block, tile_index * tiles_dev, tiles_dev, 0)
    phase_mine = lax.dynamic_slice_in_dim(phase_block, tile_index * tiles_dev, tiles_dev, 0)
    steer_re = row_steer[0]
    steer_im = row_steer[1]
    col_mine = lax.dynamic_slice_in_dim(col_steer, az_index, 1, 3)[..., 0]
    image_b = image.astype(jnp.bfloat16).reshape(2, tiles_dev, tile_rows, columns)
    image_pair = jnp.stack(
        [jnp.stack([image_b[0], image_b[1]], axis=2), jnp.stack([-image_b[1], image_b[0]], axis=2)]
    )
    prod = jnp.einsum(
        "cpjh,cjhou->pjou", row_steer, image_pair, preferred_element_type=jnp.float32
    )
    weight_re = col_mine[0][..., None]
    weight_im = col_mine[1][..., None]
    real_part = weight_re * prod[:, :, 0] - weight_im * prod[:, :, 1]
    imag_part = weight_re * prod[:, :, 1] + weight_im * prod[:, :, 0]
    parts = jnp.stack([real_part, imag_part], axis=2).reshape(az_count, -1, tiles_dev, 2, columns)
    summed = halving_sum(parts, "az", (1, 8, 2, 4))
    projection_b = jnp.transpose(summed, (1, 0, 2, 3)).astype(jnp.bfloat16)
    all_proj = doubling_gather(projection_b, "tile", (2, 1, 8, 4))
    all_proj = all_proj.reshape(-1, *all_proj.shape[2:])
    phase_ids = jnp.arange(kernels.shape[0], dtype=jnp.int32)
    my_rows = tile_index * rows_dev + jnp.arange(rows_dev, dtype=jnp.int32)
    hits = (foot_block[:, :, None, None] == my_rows[None, None, :, None]) & (
        phase_block[:, :, None, None] == phase_ids[None, None, None, :]
    )
    counts = jnp.sum(hits.astype(jnp.int32), axis=1).astype(jnp.bfloat16)
    grouped = jnp.einsum(
        "jkq,jpcu->kqpcu", counts, all_proj, preferred_element_type=jnp.float32
    )
    forward = jnp.einsum(
        "kqpcu,quv->cpkv", grouped, kernels.astype(jnp.float32), precision=highest
    )
    kern_mine = kernels[phase_mine]
    live = (aperture == 1)[None, :, None, None]
    dual_new = jnp.where(
        live,
        (data_dual + dual_step * (forward - echoes.astype(jnp.float32))) / (1.0 + dual_step),
        0.0,
    )
    dual_b = dual_new.astype(jnp.bfloat16)
    all_rows = doubling_gather(jnp.moveaxis(dual_b, 2, 0), "tile", (2, 1, 8, 4))
    all_rows = jnp.moveaxis(all_rows.reshape(-1, *all_rows.shape[2:]), 0, 2)
    chosen = jnp.take(all_rows, foot_mine, axis=2)
    back = jnp.einsum("cpjfv,jfuv->cjpu", chosen, kern_mine, preferred_element_type=jnp.float32)
    back_b = back.astype(jnp.bfloat16)
    piece = doubling_gather(jnp.moveaxis(back_b, 2, 0), "az", (4, 8, 2, 1))
    piece = jnp.moveaxis(piece.reshape(-1, *piece.shape[2:]), 0, 2)
    weight_re = col_mine[0].T[..., None]
    weight_im = col_mine[1].T[..., None]
    back_re = piece[0].astype(jnp.float32)
    back_im = piece[1].astype(jnp.float32)
    mixed_re = (weight_re * back_re + weight_im * back_im).astype(jnp.bfloat16)
    mixed_im = (weight_re * back_im - weight_im * back_re).astype(jnp.bfloat16)
    mixed = jnp.stack(
        [jnp.stack([mixed_re, mixed_im], axis=2), jnp.stack([mixed_im, -mixed_re], axis=2)]
    )
    adjoint = jnp.einsum(
        "cpjh,cjpou->ojhu", row_steer, mixed, preferred_element_type=jnp.float32
    )
    adjoint = adjoint.reshape(2, strip_rows, columns)
    stacked = jnp.concatenate([image, tv_dual.reshape(4, strip_rows, columns)], axis=0)
    padded = padded_2(stacked, (("az", 2), ("tile", 1)), 1)
    image_pad = padded[:2]
    dual_pad = padded[2:].reshape(2, 2, strip_rows + 2, columns + 2)
    total_rows = tile_count * strip_rows
    total_cols = az_count * columns
    global_row = tile_index * strip_rows - 1 + jnp.arange(strip_rows + 1, dtype=jnp.int32)
    global_col = az_index * columns - 1 + jnp.arange(columns + 1, dtype=jnp.int32)
    centre = image_pad[:, : strip_rows + 1, : columns + 1]
    grad_rows = image_pad[:, 1 : strip_rows + 2, : columns + 1] - centre
    grad_rows = jnp.where((global_row < total_rows - 1)[None, :, None], grad_rows, 0.0)
    grad_cols = image_pad[:, : strip_rows + 1, 1 : columns + 2] - centre
    grad_cols = jnp.where((global_col < total_cols - 1)[None, None, :], grad_cols, 0.0)
    moved = dual_pad[:, :, : strip_rows + 1, : columns + 1] + dual_step * jnp.stack(
        [grad_rows, grad_cols]
    )
    magnitude = jnp.sqrt(jnp.sum(moved * moved, axis=(0, 1)))
    projected = moved / jnp.maximum(1.0, magnitude / edge_limit)
    inside = (global_row >= 0)[:, None] & (global_col >= 0)[None, :]
    projected = jnp.where(inside[None, None], projected, 0.0)
    rows_part = jnp.where((global_row < total_rows - 1)[None, :, None], projected[0], 0.0)
    cols_part = jnp.where((global_col < total_cols - 1)[None, None, :], projected[1], 0.0)
    divergence = (
        rows_part[:, 1:, 1:] - rows_part[:, :-1, 1:] + cols_part[:, 1:, 1:] - cols_part[:, 1:, :-1]
    )
    image_new = image - primal_step * (adjoint - divergence)
    tv_new = projected[:, :, 1:, 1:]
    return (image_new, tv_new, dual_new)


def solution(mesh):
    in_specs = (
        P(None, "tile", "az"),
        P(None, None, "tile", "az"),
        P(None, "az", "tile", None),
        P(None, "az", "tile", None),
        P(None, None, "tile", None),
        P(None, None, "tile", None),
        P(),
        P(None, "az", None),
        P(None, "az", None),
        P("az"),
    )
    out_specs = (P(None, "tile", "az"), P(None, None, "tile", "az"), P(None, "az", "tile", None))
    return jax.shard_map(
        on_device, mesh=mesh, in_specs=in_specs, out_specs=out_specs, check_vma=False
    )
```

```python
import jax
import jax.numpy as jnp
from jax import lax
from jax.sharding import PartitionSpec as P

dual_step = 0.5
primal_step = 0.25
edge_limit = 1.5


def padded_2(block, sides, width):
    for axis, dim in sides:
        count = lax.axis_size(axis)
        forward = [(i, i + 1) for i in range(count - 1)]
        backward = [(target, source) for source, target in forward]
        low = lax.ppermute(
            lax.slice_in_dim(block, block.shape[dim] - width, None, axis=dim), axis, forward
        )
        high = lax.ppermute(lax.slice_in_dim(block, 0, width, axis=dim), axis, backward)
        block = jnp.concatenate([low, block, high], axis=dim)
    return block


def halving_sum(blocks, axis, bits):
    me = lax.axis_index(axis)
    count = lax.axis_size(axis)
    order = [count >> (level + 1) for level in range(count.bit_length() - 1)]
    blocks = blocks.reshape(*([2] * len(order)), *blocks.shape[1:])
    for bit in bits:
        place = order.index(bit)
        order.pop(place)
        mine = (me // bit) % 2
        keep = lax.dynamic_index_in_dim(blocks, mine, place, keepdims=False)
        send = lax.dynamic_index_in_dim(blocks, 1 - mine, place, keepdims=False)
        pairs = [(i, i ^ bit) for i in range(count)]
        blocks = keep + lax.ppermute(send, axis, pairs)
    return blocks


def doubling_gather(block, axis, bits):
    me = lax.axis_index(axis)
    count = lax.axis_size(axis)
    done = []
    for bit in bits:
        mine = (me // bit) % 2
        pairs = [(i, i ^ bit) for i in range(count)]
        got = lax.ppermute(block, axis, pairs)
        place = sum(1 for other in done if other > bit)
        low = jnp.where(mine == 0, block, got)
        high = jnp.where(mine == 0, got, block)
        block = jnp.stack([low, high], axis=place)
        done.append(bit)
    return block.reshape(-1, *block.shape[len(bits):])


def on_device(
    image, tv_dual, data_dual, echoes, row_steer, col_steer, kernels, footprint, phase, aperture
):
    highest = lax.Precision.HIGHEST
    az_index = lax.axis_index("az")
    tile_index = lax.axis_index("tile")
    az_count = lax.axis_size("az")
    tile_count = lax.axis_size("tile")
    strip_rows = image.shape[1]
    columns = image.shape[2]
    tiles_dev = row_steer.shape[2]
    tile_rows = row_steer.shape[3]
    rows_dev = data_dual.shape[2]
    range_rows = rows_dev * tile_count
    foot_block = footprint[:, 0, :]
    phase_block = phase[:, 0, :]
    foot_mine = lax.dynamic_slice_in_dim(foot_block, tile_index * tiles_dev, tiles_dev, 0)
    phase_mine = lax.dynamic_slice_in_dim(phase_block, tile_index * tiles_dev, tiles_dev, 0)
    steer_re = row_steer[0]
    steer_im = row_steer[1]
    col_mine = lax.dynamic_slice_in_dim(col_steer, az_index, 1, 3)[..., 0]
    image_b = image.astype(jnp.bfloat16).reshape(2, tiles_dev, tile_rows, columns)
    part_sre = steer_re
    part_sim = steer_im
    weight_re = col_mine[0][..., None]
    weight_im = col_mine[1][..., None]
    prod_re = jnp.einsum("pjh,jhu->pju", part_sre, image_b[0], preferred_element_type=jnp.float32)
    prod_re = prod_re - jnp.einsum(
        "pjh,jhu->pju", part_sim, image_b[1], preferred_element_type=jnp.float32
    )
    prod_im = jnp.einsum("pjh,jhu->pju", part_sre, image_b[1], preferred_element_type=jnp.float32)
    prod_im = prod_im + jnp.einsum(
        "pjh,jhu->pju", part_sim, image_b[0], preferred_element_type=jnp.float32
    )
    real_part = weight_re * prod_re - weight_im * prod_im
    imag_part = weight_re * prod_im + weight_im * prod_re
    parts = jnp.stack([real_part, imag_part], axis=0).reshape(2, az_count, -1, tiles_dev, columns)
    summed = halving_sum(jnp.moveaxis(parts, 1, 0), "az", (1, 8, 2, 4))
    projection_b = jnp.transpose(summed, (2, 1, 0, 3)).astype(jnp.bfloat16)
    all_proj = doubling_gather(projection_b, "tile", (2, 1, 8, 4))
    all_proj = all_proj.reshape(-1, *all_proj.shape[2:])
    phase_ids = jnp.arange(kernels.shape[0], dtype=jnp.int32)
    my_rows = tile_index * rows_dev + jnp.arange(rows_dev, dtype=jnp.int32)
    hits = (foot_block[:, :, None, None] == my_rows[None, None, :, None]) & (
        phase_block[:, :, None, None] == phase_ids[None, None, None, :]
    )
    counts = jnp.sum(hits.astype(jnp.int32), axis=1).astype(jnp.bfloat16)
    grouped = jnp.einsum(
        "jkq,jpcu->kqpcu", counts, all_proj, preferred_element_type=jnp.float32
    )
    forward = jnp.einsum(
        "kqpcu,quv->cpkv", grouped, kernels.astype(jnp.float32), precision=highest
    )
    kern_mine = kernels[phase_mine]
    live = (aperture == 1)[None, :, None, None]
    dual_new = jnp.where(
        live,
        (data_dual + dual_step * (forward - echoes.astype(jnp.float32))) / (1.0 + dual_step),
        0.0,
    )
    dual_b = dual_new.astype(jnp.bfloat16)
    all_rows = doubling_gather(jnp.moveaxis(dual_b, 2, 0), "tile", (2, 1, 8, 4))
    all_rows = jnp.moveaxis(all_rows.reshape(-1, *all_rows.shape[2:]), 0, 2)
    chosen = jnp.take(all_rows, foot_mine, axis=2)
    back = jnp.einsum("cpjfv,jfuv->cjpu", chosen, kern_mine, preferred_element_type=jnp.float32)
    back_b = back.astype(jnp.bfloat16)
    near = doubling_gather(jnp.moveaxis(back_b, 2, 0), "az", (4, 8, 2))
    core = az_index % 2
    far = lax.ppermute(near, "az", [(i, i ^ 1) for i in range(az_count)])
    block_pulses = back_b.shape[2]
    steer_split = row_steer.reshape(2, az_count // 2, 2, block_pulses, tiles_dev, tile_rows)
    col_split = col_mine.reshape(2, az_count // 2, 2, block_pulses, tiles_dev)

    def partial_adjoint(blocks, side):
        piece = jnp.transpose(blocks, (2, 3, 0, 1, 4))
        steer = lax.dynamic_index_in_dim(steer_split, side, 2, keepdims=False)
        cols = lax.dynamic_index_in_dim(col_split, side, 2, keepdims=False)
        weight_re = jnp.transpose(cols[0], (2, 0, 1))[..., None]
        weight_im = jnp.transpose(cols[1], (2, 0, 1))[..., None]
        back_re = piece[0].astype(jnp.float32)
        back_im = piece[1].astype(jnp.float32)
        mixed_re = (weight_re * back_re + weight_im * back_im).astype(jnp.bfloat16)
        mixed_im = (weight_re * back_im - weight_im * back_re).astype(jnp.bfloat16)
        grad_re = jnp.einsum(
            "bpjh,jbpu->jhu", steer[0], mixed_re, preferred_element_type=jnp.float32
        ) + jnp.einsum("bpjh,jbpu->jhu", steer[1], mixed_im, preferred_element_type=jnp.float32)
        grad_im = jnp.einsum(
            "bpjh,jbpu->jhu", steer[0], mixed_im, preferred_element_type=jnp.float32
        ) - jnp.einsum("bpjh,jbpu->jhu", steer[1], mixed_re, preferred_element_type=jnp.float32)
        return jnp.stack([grad_re, grad_im])

    adjoint = partial_adjoint(near, core) + partial_adjoint(far, 1 - core)
    adjoint = adjoint.reshape(2, strip_rows, columns)
    stacked = jnp.concatenate([image, tv_dual.reshape(4, strip_rows, columns)], axis=0)
    padded = padded_2(stacked, (("az", 2), ("tile", 1)), 1)
    image_pad = padded[:2]
    dual_pad = padded[2:].reshape(2, 2, strip_rows + 2, columns + 2)
    total_rows = tile_count * strip_rows
    total_cols = az_count * columns
    global_row = tile_index * strip_rows - 1 + jnp.arange(strip_rows + 1, dtype=jnp.int32)
    global_col = az_index * columns - 1 + jnp.arange(columns + 1, dtype=jnp.int32)
    centre = image_pad[:, : strip_rows + 1, : columns + 1]
    grad_rows = image_pad[:, 1 : strip_rows + 2, : columns + 1] - centre
    grad_rows = jnp.where((global_row < total_rows - 1)[None, :, None], grad_rows, 0.0)
    grad_cols = image_pad[:, : strip_rows + 1, 1 : columns + 2] - centre
    grad_cols = jnp.where((global_col < total_cols - 1)[None, None, :], grad_cols, 0.0)
    moved = dual_pad[:, :, : strip_rows + 1, : columns + 1] + dual_step * jnp.stack(
        [grad_rows, grad_cols]
    )
    magnitude = jnp.sqrt(jnp.sum(moved * moved, axis=(0, 1)))
    projected = moved / jnp.maximum(1.0, magnitude / edge_limit)
    inside = (global_row >= 0)[:, None] & (global_col >= 0)[None, :]
    projected = jnp.where(inside[None, None], projected, 0.0)
    rows_part = jnp.where((global_row < total_rows - 1)[None, :, None], projected[0], 0.0)
    cols_part = jnp.where((global_col < total_cols - 1)[None, None, :], projected[1], 0.0)
    divergence = (
        rows_part[:, 1:, 1:] - rows_part[:, :-1, 1:] + cols_part[:, 1:, 1:] - cols_part[:, 1:, :-1]
    )
    image_new = image - primal_step * (adjoint - divergence)
    tv_new = projected[:, :, 1:, 1:]
    return (image_new, tv_new, dual_new)


def solution(mesh):
    in_specs = (
        P(None, "tile", "az"),
        P(None, None, "tile", "az"),
        P(None, "az", "tile", None),
        P(None, "az", "tile", None),
        P(None, None, "tile", None),
        P(None, None, "tile", None),
        P(),
        P(None, "az", None),
        P(None, "az", None),
        P("az"),
    )
    out_specs = (P(None, "tile", "az"), P(None, None, "tile", "az"), P(None, "az", "tile", None))
    return jax.shard_map(
        on_device, mesh=mesh, in_specs=in_specs, out_specs=out_specs, check_vma=False
    )
```

```python
import jax
import jax.numpy as jnp
from jax import lax
from jax.sharding import PartitionSpec as P

dual_step = 0.5
primal_step = 0.25
edge_limit = 1.5


def padded_2(block, sides, width):
    for axis, dim in sides:
        count = lax.axis_size(axis)
        forward = [(i, i + 1) for i in range(count - 1)]
        backward = [(target, source) for source, target in forward]
        low = lax.ppermute(
            lax.slice_in_dim(block, block.shape[dim] - width, None, axis=dim), axis, forward
        )
        high = lax.ppermute(lax.slice_in_dim(block, 0, width, axis=dim), axis, backward)
        block = jnp.concatenate([low, block, high], axis=dim)
    return block


def halving_sum(blocks, axis, bits):
    me = lax.axis_index(axis)
    count = lax.axis_size(axis)
    order = [count >> (level + 1) for level in range(count.bit_length() - 1)]
    blocks = blocks.reshape(*([2] * len(order)), *blocks.shape[1:])
    for bit in bits:
        place = order.index(bit)
        order.pop(place)
        mine = (me // bit) % 2
        keep = lax.dynamic_index_in_dim(blocks, mine, place, keepdims=False)
        send = lax.dynamic_index_in_dim(blocks, 1 - mine, place, keepdims=False)
        pairs = [(i, i ^ bit) for i in range(count)]
        blocks = keep + lax.ppermute(send, axis, pairs)
    return blocks


def doubling_gather(block, axis, bits):
    me = lax.axis_index(axis)
    count = lax.axis_size(axis)
    done = []
    for bit in bits:
        mine = (me // bit) % 2
        pairs = [(i, i ^ bit) for i in range(count)]
        got = lax.ppermute(block, axis, pairs)
        place = sum(1 for other in done if other > bit)
        low = jnp.where(mine == 0, block, got)
        high = jnp.where(mine == 0, got, block)
        block = jnp.stack([low, high], axis=place)
        done.append(bit)
    return block.reshape(count, *block.shape[len(bits):])


def on_device(
    image, tv_dual, data_dual, echoes, row_steer, col_steer, kernels, footprint, phase, aperture
):
    highest = lax.Precision.HIGHEST
    az_index = lax.axis_index("az")
    tile_index = lax.axis_index("tile")
    az_count = lax.axis_size("az")
    tile_count = lax.axis_size("tile")
    strip_rows = image.shape[1]
    columns = image.shape[2]
    tiles_dev = row_steer.shape[2]
    tile_rows = row_steer.shape[3]
    rows_dev = data_dual.shape[2]
    range_rows = rows_dev * tile_count
    foot_block = footprint[:, 0, :]
    phase_block = phase[:, 0, :]
    foot_mine = lax.dynamic_slice_in_dim(foot_block, tile_index * tiles_dev, tiles_dev, 0)
    phase_mine = lax.dynamic_slice_in_dim(phase_block, tile_index * tiles_dev, tiles_dev, 0)
    steer_re = row_steer[0]
    steer_im = row_steer[1]
    col_mine = lax.dynamic_slice_in_dim(col_steer, az_index, 1, 3)[..., 0]
    image_b = image.astype(jnp.bfloat16).reshape(2, tiles_dev, tile_rows, columns)
    part_sre = steer_re
    part_sim = steer_im
    weight_re = col_mine[0][..., None]
    weight_im = col_mine[1][..., None]
    prod_re = jnp.einsum("pjh,jhu->pju", part_sre, image_b[0], preferred_element_type=jnp.float32)
    prod_re = prod_re - jnp.einsum(
        "pjh,jhu->pju", part_sim, image_b[1], preferred_element_type=jnp.float32
    )
    prod_im = jnp.einsum("pjh,jhu->pju", part_sre, image_b[1], preferred_element_type=jnp.float32)
    prod_im = prod_im + jnp.einsum(
        "pjh,jhu->pju", part_sim, image_b[0], preferred_element_type=jnp.float32
    )
    real_part = weight_re * prod_re - weight_im * prod_im
    imag_part = weight_re * prod_im + weight_im * prod_re
    parts = jnp.stack([real_part, imag_part], axis=0).reshape(2, az_count, -1, tiles_dev, columns)
    stacked = jnp.concatenate([image, tv_dual.reshape(4, strip_rows, columns)], axis=0)
    padded = padded_2(stacked, (("az", 2), ("tile", 1)), 1)
    padded, parts = lax.optimization_barrier((padded, parts))
    summed = halving_sum(jnp.moveaxis(parts, 1, 0), "az", (1, 8, 2, 4))
    projection_b = jnp.transpose(summed, (2, 1, 0, 3)).astype(jnp.bfloat16)
    all_proj = doubling_gather(projection_b, "tile", (2, 1, 8, 4))
    all_proj = all_proj.reshape(-1, *all_proj.shape[2:])
    phase_ids = jnp.arange(kernels.shape[0], dtype=jnp.int32)
    my_rows = tile_index * rows_dev + jnp.arange(rows_dev, dtype=jnp.int32)
    hits = (foot_block[:, :, None, None] == my_rows[None, None, :, None]) & (
        phase_block[:, :, None, None] == phase_ids[None, None, None, :]
    )
    counts = jnp.sum(hits.astype(jnp.int32), axis=1).astype(jnp.bfloat16)
    grouped = jnp.einsum(
        "jkq,jpcu->kqpcu", counts, all_proj, preferred_element_type=jnp.float32
    )
    forward = jnp.einsum(
        "kqpcu,quv->cpkv", grouped, kernels.astype(jnp.float32), precision=highest
    )
    kern_mine = kernels[phase_mine]
    live = (aperture == 1)[None, :, None, None]
    dual_new = jnp.where(
        live,
        (data_dual + dual_step * (forward - echoes.astype(jnp.float32))) / (1.0 + dual_step),
        0.0,
    )
    dual_b = dual_new.astype(jnp.bfloat16)
    all_rows = doubling_gather(jnp.moveaxis(dual_b, 2, 0), "tile", (2, 1, 8, 4))
    all_rows = jnp.moveaxis(all_rows.reshape(-1, *all_rows.shape[2:]), 0, 2)
    chosen = jnp.take(all_rows, foot_mine, axis=2)
    back = jnp.einsum("cpjfv,jfuv->cjpu", chosen, kern_mine, preferred_element_type=jnp.float32)
    back_b = back.astype(jnp.bfloat16)
    piece = doubling_gather(jnp.moveaxis(back_b, 2, 0), "az", (4, 8, 2, 1))
    piece = jnp.moveaxis(piece.reshape(-1, *piece.shape[2:]), 0, 2)
    weight_re = col_mine[0].T[..., None]
    weight_im = col_mine[1].T[..., None]
    back_re = piece[0].astype(jnp.float32)
    back_im = piece[1].astype(jnp.float32)
    mixed_re = (weight_re * back_re + weight_im * back_im).astype(jnp.bfloat16)
    mixed_im = (weight_re * back_im - weight_im * back_re).astype(jnp.bfloat16)
    part_sre = steer_re
    part_sim = steer_im
    grad_re = jnp.einsum("pjh,jpu->jhu", part_sre, mixed_re, preferred_element_type=jnp.float32)
    grad_re = grad_re + jnp.einsum(
        "pjh,jpu->jhu", part_sim, mixed_im, preferred_element_type=jnp.float32
    )
    grad_im = jnp.einsum("pjh,jpu->jhu", part_sre, mixed_im, preferred_element_type=jnp.float32)
    grad_im = grad_im - jnp.einsum(
        "pjh,jpu->jhu", part_sim, mixed_re, preferred_element_type=jnp.float32
    )
    adjoint = jnp.stack([grad_re, grad_im])
    adjoint = adjoint.reshape(2, strip_rows, columns)
    image_pad = padded[:2]
    dual_pad = padded[2:].reshape(2, 2, strip_rows + 2, columns + 2)
    total_rows = tile_count * strip_rows
    total_cols = az_count * columns
    global_row = tile_index * strip_rows - 1 + jnp.arange(strip_rows + 1, dtype=jnp.int32)
    global_col = az_index * columns - 1 + jnp.arange(columns + 1, dtype=jnp.int32)
    centre = image_pad[:, : strip_rows + 1, : columns + 1]
    grad_rows = image_pad[:, 1 : strip_rows + 2, : columns + 1] - centre
    grad_rows = jnp.where((global_row < total_rows - 1)[None, :, None], grad_rows, 0.0)
    grad_cols = image_pad[:, : strip_rows + 1, 1 : columns + 2] - centre
    grad_cols = jnp.where((global_col < total_cols - 1)[None, None, :], grad_cols, 0.0)
    moved = dual_pad[:, :, : strip_rows + 1, : columns + 1] + dual_step * jnp.stack(
        [grad_rows, grad_cols]
    )
    magnitude = jnp.sqrt(jnp.sum(moved * moved, axis=(0, 1)))
    projected = moved / jnp.maximum(1.0, magnitude / edge_limit)
    inside = (global_row >= 0)[:, None] & (global_col >= 0)[None, :]
    projected = jnp.where(inside[None, None], projected, 0.0)
    rows_part = jnp.where((global_row < total_rows - 1)[None, :, None], projected[0], 0.0)
    cols_part = jnp.where((global_col < total_cols - 1)[None, None, :], projected[1], 0.0)
    divergence = (
        rows_part[:, 1:, 1:] - rows_part[:, :-1, 1:] + cols_part[:, 1:, 1:] - cols_part[:, 1:, :-1]
    )
    image_new = image - primal_step * (adjoint - divergence)
    tv_new = projected[:, :, 1:, 1:]
    return (image_new, tv_new, dual_new)


def solution(mesh):
    in_specs = (
        P(None, "tile", "az"),
        P(None, None, "tile", "az"),
        P(None, "az", "tile", None),
        P(None, "az", "tile", None),
        P(None, None, "tile", None),
        P(None, None, "tile", None),
        P(),
        P(None, "az", None),
        P(None, "az", None),
        P("az"),
    )
    out_specs = (P(None, "tile", "az"), P(None, None, "tile", "az"), P(None, "az", "tile", None))
    return jax.shard_map(
        on_device, mesh=mesh, in_specs=in_specs, out_specs=out_specs, check_vma=False
    )
```

```python
import jax
import jax.numpy as jnp
from jax import lax
from jax.sharding import PartitionSpec as P

dual_step = 0.5
primal_step = 0.25
edge_limit = 1.5


def padded_2(block, sides, width):
    for axis, dim in sides:
        count = lax.axis_size(axis)
        forward = [(i, i + 1) for i in range(count - 1)]
        backward = [(target, source) for source, target in forward]
        low = lax.ppermute(
            lax.slice_in_dim(block, block.shape[dim] - width, None, axis=dim), axis, forward
        )
        high = lax.ppermute(lax.slice_in_dim(block, 0, width, axis=dim), axis, backward)
        block = jnp.concatenate([low, block, high], axis=dim)
    return block


def halving_sum(blocks, axis, bits):
    me = lax.axis_index(axis)
    count = lax.axis_size(axis)
    order = [count >> (level + 1) for level in range(count.bit_length() - 1)]
    blocks = blocks.reshape(*([2] * len(order)), *blocks.shape[1:])
    for bit in bits:
        place = order.index(bit)
        order.pop(place)
        mine = (me // bit) % 2
        keep = lax.dynamic_index_in_dim(blocks, mine, place, keepdims=False)
        send = lax.dynamic_index_in_dim(blocks, 1 - mine, place, keepdims=False)
        pairs = [(i, i ^ bit) for i in range(count)]
        blocks = keep + lax.ppermute(send, axis, pairs)
    return blocks


def doubling_gather(block, axis, bits):
    me = lax.axis_index(axis)
    count = lax.axis_size(axis)
    done = []
    for bit in bits:
        mine = (me // bit) % 2
        pairs = [(i, i ^ bit) for i in range(count)]
        got = lax.ppermute(block, axis, pairs)
        place = sum(1 for other in done if other > bit)
        low = jnp.where(mine == 0, block, got)
        high = jnp.where(mine == 0, got, block)
        block = jnp.stack([low, high], axis=place)
        done.append(bit)
    return block.reshape(count, *block.shape[len(bits):])


def on_device(
    image, tv_dual, data_dual, echoes, row_steer, col_steer, kernels, footprint, phase, aperture
):
    highest = lax.Precision.HIGHEST
    az_index = lax.axis_index("az")
    tile_index = lax.axis_index("tile")
    az_count = lax.axis_size("az")
    tile_count = lax.axis_size("tile")
    strip_rows = image.shape[1]
    columns = image.shape[2]
    tiles_dev = row_steer.shape[2]
    tile_rows = row_steer.shape[3]
    rows_dev = data_dual.shape[2]
    range_rows = rows_dev * tile_count
    foot_block = footprint[:, 0, :]
    phase_block = phase[:, 0, :]
    foot_mine = lax.dynamic_slice_in_dim(foot_block, tile_index * tiles_dev, tiles_dev, 0)
    phase_mine = lax.dynamic_slice_in_dim(phase_block, tile_index * tiles_dev, tiles_dev, 0)
    steer_re = row_steer[0]
    steer_im = row_steer[1]
    col_mine = lax.dynamic_slice_in_dim(col_steer, az_index, 1, 3)[..., 0]
    image_b = image.astype(jnp.bfloat16).reshape(2, tiles_dev, tile_rows, columns)
    part_sre = steer_re
    part_sim = steer_im
    weight_re = col_mine[0][..., None]
    weight_im = col_mine[1][..., None]
    prod_re = jnp.einsum("pjh,jhu->pju", part_sre, image_b[0], preferred_element_type=jnp.float32)
    prod_re = prod_re - jnp.einsum(
        "pjh,jhu->pju", part_sim, image_b[1], preferred_element_type=jnp.float32
    )
    prod_im = jnp.einsum("pjh,jhu->pju", part_sre, image_b[1], preferred_element_type=jnp.float32)
    prod_im = prod_im + jnp.einsum(
        "pjh,jhu->pju", part_sim, image_b[0], preferred_element_type=jnp.float32
    )
    real_part = weight_re * prod_re - weight_im * prod_im
    imag_part = weight_re * prod_im + weight_im * prod_re
    parts = jnp.stack([real_part, imag_part], axis=0).reshape(2, az_count, -1, tiles_dev, columns)
    summed = halving_sum(jnp.moveaxis(parts, 1, 0), "az", (1, 8, 2, 4))
    projection_b = jnp.transpose(summed, (2, 1, 0, 3)).astype(jnp.bfloat16)
    all_proj = doubling_gather(projection_b, "tile", (2, 1, 8, 4))
    all_proj = all_proj.reshape(-1, *all_proj.shape[2:])
    phase_ids = jnp.arange(kernels.shape[0], dtype=jnp.int32)
    my_rows = tile_index * rows_dev + jnp.arange(rows_dev, dtype=jnp.int32)
    hits = (foot_block[:, :, None, None] == my_rows[None, None, :, None]) & (
        phase_block[:, :, None, None] == phase_ids[None, None, None, :]
    )
    counts = jnp.sum(hits.astype(jnp.int32), axis=1).astype(jnp.bfloat16)
    grouped = jnp.einsum(
        "jkq,jpcu->kqpcu", counts, all_proj, preferred_element_type=jnp.float32
    )
    forward = jnp.einsum(
        "kqpcu,quv->cpkv", grouped, kernels.astype(jnp.float32), precision=highest
    )
    kern_mine = kernels[phase_mine]
    live = (aperture == 1)[None, :, None, None]
    dual_new = jnp.where(
        live,
        (data_dual + dual_step * (forward - echoes.astype(jnp.float32))) / (1.0 + dual_step),
        0.0,
    )
    dual_b = dual_new.astype(jnp.bfloat16)
    all_rows = doubling_gather(jnp.moveaxis(dual_b, 2, 0), "tile", (2, 1, 8, 4))
    all_rows = jnp.moveaxis(all_rows.reshape(-1, *all_rows.shape[2:]), 0, 2)
    row_pick = (foot_mine[:, :, None] == jnp.arange(range_rows, dtype=jnp.int32)).astype(
        jnp.bfloat16
    )
    chosen = jnp.einsum(
        "jfk,cpkv->cpjfv", row_pick, all_rows, preferred_element_type=jnp.float32
    ).astype(jnp.bfloat16)
    back = jnp.einsum("cpjfv,jfuv->cjpu", chosen, kern_mine, preferred_element_type=jnp.float32)
    back_b = back.astype(jnp.bfloat16)
    piece = doubling_gather(jnp.moveaxis(back_b, 2, 0), "az", (4, 8, 2, 1))
    piece = jnp.moveaxis(piece.reshape(-1, *piece.shape[2:]), 0, 2)
    weight_re = col_mine[0].T[..., None]
    weight_im = col_mine[1].T[..., None]
    back_re = piece[0].astype(jnp.float32)
    back_im = piece[1].astype(jnp.float32)
    mixed_re = (weight_re * back_re + weight_im * back_im).astype(jnp.bfloat16)
    mixed_im = (weight_re * back_im - weight_im * back_re).astype(jnp.bfloat16)
    part_sre = steer_re
    part_sim = steer_im
    grad_re = jnp.einsum("pjh,jpu->jhu", part_sre, mixed_re, preferred_element_type=jnp.float32)
    grad_re = grad_re + jnp.einsum(
        "pjh,jpu->jhu", part_sim, mixed_im, preferred_element_type=jnp.float32
    )
    grad_im = jnp.einsum("pjh,jpu->jhu", part_sre, mixed_im, preferred_element_type=jnp.float32)
    grad_im = grad_im - jnp.einsum(
        "pjh,jpu->jhu", part_sim, mixed_re, preferred_element_type=jnp.float32
    )
    adjoint = jnp.stack([grad_re, grad_im])
    adjoint = adjoint.reshape(2, strip_rows, columns)
    stacked = jnp.concatenate([image, tv_dual.reshape(4, strip_rows, columns)], axis=0)
    padded = padded_2(stacked, (("az", 2), ("tile", 1)), 1)
    image_pad = padded[:2]
    dual_pad = padded[2:].reshape(2, 2, strip_rows + 2, columns + 2)
    total_rows = tile_count * strip_rows
    total_cols = az_count * columns
    global_row = tile_index * strip_rows - 1 + jnp.arange(strip_rows + 1, dtype=jnp.int32)
    global_col = az_index * columns - 1 + jnp.arange(columns + 1, dtype=jnp.int32)
    centre = image_pad[:, : strip_rows + 1, : columns + 1]
    grad_rows = image_pad[:, 1 : strip_rows + 2, : columns + 1] - centre
    grad_rows = jnp.where((global_row < total_rows - 1)[None, :, None], grad_rows, 0.0)
    grad_cols = image_pad[:, : strip_rows + 1, 1 : columns + 2] - centre
    grad_cols = jnp.where((global_col < total_cols - 1)[None, None, :], grad_cols, 0.0)
    moved = dual_pad[:, :, : strip_rows + 1, : columns + 1] + dual_step * jnp.stack(
        [grad_rows, grad_cols]
    )
    magnitude = jnp.sqrt(jnp.sum(moved * moved, axis=(0, 1)))
    projected = moved / jnp.maximum(1.0, magnitude / edge_limit)
    inside = (global_row >= 0)[:, None] & (global_col >= 0)[None, :]
    projected = jnp.where(inside[None, None], projected, 0.0)
    rows_part = jnp.where((global_row < total_rows - 1)[None, :, None], projected[0], 0.0)
    cols_part = jnp.where((global_col < total_cols - 1)[None, None, :], projected[1], 0.0)
    divergence = (
        rows_part[:, 1:, 1:] - rows_part[:, :-1, 1:] + cols_part[:, 1:, 1:] - cols_part[:, 1:, :-1]
    )
    image_new = image - primal_step * (adjoint - divergence)
    tv_new = projected[:, :, 1:, 1:]
    return (image_new, tv_new, dual_new)


def solution(mesh):
    in_specs = (
        P(None, "tile", "az"),
        P(None, None, "tile", "az"),
        P(None, "az", "tile", None),
        P(None, "az", "tile", None),
        P(None, None, "tile", None),
        P(None, None, "tile", None),
        P(),
        P(None, "az", None),
        P(None, "az", None),
        P("az"),
    )
    out_specs = (P(None, "tile", "az"), P(None, None, "tile", "az"), P(None, "az", "tile", None))
    return jax.shard_map(
        on_device, mesh=mesh, in_specs=in_specs, out_specs=out_specs, check_vma=False
    )
```

```python
import jax
import jax.numpy as jnp
from jax import lax
from jax.sharding import PartitionSpec as P

dual_step = 0.5
primal_step = 0.25
edge_limit = 1.5


def padded_2(block, sides, width):
    for axis, dim in sides:
        count = lax.axis_size(axis)
        forward = [(i, i + 1) for i in range(count - 1)]
        backward = [(target, source) for source, target in forward]
        low = lax.ppermute(
            lax.slice_in_dim(block, block.shape[dim] - width, None, axis=dim), axis, forward
        )
        high = lax.ppermute(lax.slice_in_dim(block, 0, width, axis=dim), axis, backward)
        block = jnp.concatenate([low, block, high], axis=dim)
    return block


def halving_sum(blocks, axis, bits):
    me = lax.axis_index(axis)
    count = lax.axis_size(axis)
    order = [count >> (level + 1) for level in range(count.bit_length() - 1)]
    blocks = blocks.reshape(*([2] * len(order)), *blocks.shape[1:])
    for bit in bits:
        place = order.index(bit)
        order.pop(place)
        mine = (me // bit) % 2
        keep = lax.dynamic_index_in_dim(blocks, mine, place, keepdims=False)
        send = lax.dynamic_index_in_dim(blocks, 1 - mine, place, keepdims=False)
        pairs = [(i, i ^ bit) for i in range(count)]
        blocks = keep + lax.ppermute(send, axis, pairs)
    return blocks


def doubling_gather(block, axis, bits):
    me = lax.axis_index(axis)
    count = lax.axis_size(axis)
    done = []
    for bit in bits:
        mine = (me // bit) % 2
        pairs = [(i, i ^ bit) for i in range(count)]
        got = lax.ppermute(block, axis, pairs)
        place = sum(1 for other in done if other > bit)
        low = jnp.where(mine == 0, block, got)
        high = jnp.where(mine == 0, got, block)
        block = jnp.stack([low, high], axis=place)
        done.append(bit)
    return block.reshape(count, *block.shape[len(bits):])


def on_device(
    image, tv_dual, data_dual, echoes, row_steer, col_steer, kernels, footprint, phase, aperture
):
    highest = lax.Precision.HIGHEST
    az_index = lax.axis_index("az")
    tile_index = lax.axis_index("tile")
    az_count = lax.axis_size("az")
    tile_count = lax.axis_size("tile")
    strip_rows = image.shape[1]
    columns = image.shape[2]
    tiles_dev = row_steer.shape[2]
    tile_rows = row_steer.shape[3]
    rows_dev = data_dual.shape[2]
    range_rows = rows_dev * tile_count
    foot_block = footprint[:, 0, :]
    phase_block = phase[:, 0, :]
    foot_mine = lax.dynamic_slice_in_dim(foot_block, tile_index * tiles_dev, tiles_dev, 0)
    phase_mine = lax.dynamic_slice_in_dim(phase_block, tile_index * tiles_dev, tiles_dev, 0)
    steer_re = row_steer[0]
    steer_im = row_steer[1]
    col_mine = lax.dynamic_slice_in_dim(col_steer, az_index, 1, 3)[..., 0]
    image_b = image.astype(jnp.bfloat16).reshape(2, tiles_dev, tile_rows, columns)
    part_sre = steer_re
    part_sim = steer_im
    weight_re = col_mine[0][..., None]
    weight_im = col_mine[1][..., None]
    prod_re = jnp.einsum("pjh,jhu->pju", part_sre, image_b[0], preferred_element_type=jnp.float32)
    prod_re = prod_re - jnp.einsum(
        "pjh,jhu->pju", part_sim, image_b[1], preferred_element_type=jnp.float32
    )
    prod_im = jnp.einsum("pjh,jhu->pju", part_sre, image_b[1], preferred_element_type=jnp.float32)
    prod_im = prod_im + jnp.einsum(
        "pjh,jhu->pju", part_sim, image_b[0], preferred_element_type=jnp.float32
    )
    real_part = weight_re * prod_re - weight_im * prod_im
    imag_part = weight_re * prod_im + weight_im * prod_re
    parts = jnp.stack([real_part, imag_part], axis=0).reshape(2, az_count, -1, tiles_dev, columns)
    summed = halving_sum(jnp.moveaxis(parts, 1, 0), "az", (1, 8, 2, 4))
    projection_b = jnp.transpose(summed, (2, 1, 0, 3)).astype(jnp.bfloat16)
    all_proj = doubling_gather(projection_b, "tile", (2, 1, 8, 4))
    all_proj = all_proj.reshape(-1, *all_proj.shape[2:])
    phase_ids = jnp.arange(kernels.shape[0], dtype=jnp.int32)
    my_rows = tile_index * rows_dev + jnp.arange(rows_dev, dtype=jnp.int32)
    hits = (foot_block[:, :, None, None] == my_rows[None, None, :, None]) & (
        phase_block[:, :, None, None] == phase_ids[None, None, None, :]
    )
    counts = jnp.sum(hits.astype(jnp.int32), axis=1).astype(jnp.bfloat16)
    grouped = jnp.einsum(
        "jkq,jpcu->kqpcu", counts, all_proj, preferred_element_type=jnp.float32
    )
    forward = jnp.einsum(
        "kqpcu,quv->cpkv", grouped, kernels.astype(jnp.float32), precision=highest
    )
    kern_mine = kernels[phase_mine]
    live = (aperture == 1)[None, :, None, None]
    dual_new = jnp.where(
        live,
        (data_dual + dual_step * (forward - echoes.astype(jnp.float32))) / (1.0 + dual_step),
        0.0,
    )
    dual_b = dual_new.astype(jnp.bfloat16)
    all_rows = doubling_gather(jnp.moveaxis(dual_b, 2, 0), "tile", (2, 1, 8, 4))
    all_rows = jnp.moveaxis(all_rows.reshape(-1, *all_rows.shape[2:]), 0, 2)
    row_pick = (foot_mine[:, :, None] == jnp.arange(range_rows, dtype=jnp.int32)).astype(
        jnp.bfloat16
    )
    chosen = jnp.einsum(
        "jfk,cpkv->cpjfv", row_pick, all_rows, preferred_element_type=jnp.float32
    ).astype(jnp.bfloat16)
    back = jnp.einsum("cpjfv,jfuv->cjpu", chosen, kern_mine, preferred_element_type=jnp.float32)
    back_b = back.astype(jnp.bfloat16)
    piece = doubling_gather(jnp.moveaxis(back_b, 2, 0), "az", (4, 8, 2, 1))
    piece = jnp.moveaxis(piece.reshape(-1, *piece.shape[2:]), 0, 2)
    weight_re = col_mine[0].T[..., None]
    weight_im = col_mine[1].T[..., None]
    back_re = piece[0].astype(jnp.float32)
    back_im = piece[1].astype(jnp.float32)
    mixed_re = (weight_re * back_re + weight_im * back_im).astype(jnp.bfloat16)
    mixed_im = (weight_re * back_im - weight_im * back_re).astype(jnp.bfloat16)
    part_sre = steer_re
    part_sim = steer_im
    grad_re = jnp.einsum("pjh,jpu->jhu", part_sre, mixed_re, preferred_element_type=jnp.float32)
    grad_re = grad_re + jnp.einsum(
        "pjh,jpu->jhu", part_sim, mixed_im, preferred_element_type=jnp.float32
    )
    grad_im = jnp.einsum("pjh,jpu->jhu", part_sre, mixed_im, preferred_element_type=jnp.float32)
    grad_im = grad_im - jnp.einsum(
        "pjh,jpu->jhu", part_sim, mixed_re, preferred_element_type=jnp.float32
    )
    adjoint = jnp.stack([grad_re, grad_im])
    adjoint = adjoint.reshape(2, strip_rows, columns)
    total_rows = tile_count * strip_rows
    total_cols = az_count * columns
    global_row = tile_index * strip_rows + jnp.arange(strip_rows, dtype=jnp.int32)
    global_col = az_index * columns + jnp.arange(columns, dtype=jnp.int32)
    last_row = (global_row == total_rows - 1)[None, :, None]
    last_col = (global_col == total_cols - 1)[None, None, :]
    up_tile = [(i + 1, i) for i in range(tile_count - 1)]
    up_az = [(i + 1, i) for i in range(az_count - 1)]
    next_row = lax.ppermute(image[:, :1, :], "tile", up_tile)
    next_col = lax.ppermute(image[:, :, :1], "az", up_az)
    grad_rows = jnp.concatenate([image[:, 1:, :], next_row], axis=1) - image
    grad_rows = jnp.where(last_row, 0.0, grad_rows)
    grad_cols = jnp.concatenate([image[:, :, 1:], next_col], axis=2) - image
    grad_cols = jnp.where(last_col, 0.0, grad_cols)
    moved = tv_dual + dual_step * jnp.stack([grad_rows, grad_cols])
    magnitude = jnp.sqrt(jnp.sum(moved * moved, axis=(0, 1)))
    tv_new = moved / jnp.maximum(1.0, magnitude / edge_limit)
    rows_part = jnp.where(last_row, 0.0, tv_new[0])
    cols_part = jnp.where(last_col, 0.0, tv_new[1])
    down_tile = [(i, i + 1) for i in range(tile_count - 1)]
    down_az = [(i, i + 1) for i in range(az_count - 1)]
    prev_row = lax.ppermute(rows_part[:, -1:, :], "tile", down_tile)
    prev_col = lax.ppermute(cols_part[:, :, -1:], "az", down_az)
    divergence = (
        rows_part
        - jnp.concatenate([prev_row, rows_part[:, :-1, :]], axis=1)
        + cols_part
        - jnp.concatenate([prev_col, cols_part[:, :, :-1]], axis=2)
    )
    image_new = image - primal_step * (adjoint - divergence)
    return (image_new, tv_new, dual_new)


def solution(mesh):
    in_specs = (
        P(None, "tile", "az"),
        P(None, None, "tile", "az"),
        P(None, "az", "tile", None),
        P(None, "az", "tile", None),
        P(None, None, "tile", None),
        P(None, None, "tile", None),
        P(),
        P(None, "az", None),
        P(None, "az", None),
        P("az"),
    )
    out_specs = (P(None, "tile", "az"), P(None, None, "tile", "az"), P(None, "az", "tile", None))
    return jax.shard_map(
        on_device, mesh=mesh, in_specs=in_specs, out_specs=out_specs, check_vma=False
    )
```

```python
import jax
import jax.numpy as jnp
from jax import lax
from jax.sharding import PartitionSpec as P

dual_step = 0.5
primal_step = 0.25
edge_limit = 1.5


def padded_2(block, sides, width):
    for axis, dim in sides:
        count = lax.axis_size(axis)
        forward = [(i, i + 1) for i in range(count - 1)]
        backward = [(target, source) for source, target in forward]
        low = lax.ppermute(
            lax.slice_in_dim(block, block.shape[dim] - width, None, axis=dim), axis, forward
        )
        high = lax.ppermute(lax.slice_in_dim(block, 0, width, axis=dim), axis, backward)
        block = jnp.concatenate([low, block, high], axis=dim)
    return block


def halving_sum(blocks, axis, bits):
    me = lax.axis_index(axis)
    count = lax.axis_size(axis)
    order = [count >> (level + 1) for level in range(count.bit_length() - 1)]
    blocks = blocks.reshape(*([2] * len(order)), *blocks.shape[1:])
    for bit in bits:
        place = order.index(bit)
        order.pop(place)
        mine = (me // bit) % 2
        keep = lax.dynamic_index_in_dim(blocks, mine, place, keepdims=False)
        send = lax.dynamic_index_in_dim(blocks, 1 - mine, place, keepdims=False)
        pairs = [(i, i ^ bit) for i in range(count)]
        blocks = keep + lax.ppermute(send, axis, pairs)
    return blocks


def doubling_gather(block, axis, bits):
    me = lax.axis_index(axis)
    count = lax.axis_size(axis)
    done = []
    for bit in bits:
        mine = (me // bit) % 2
        pairs = [(i, i ^ bit) for i in range(count)]
        got = lax.ppermute(block, axis, pairs)
        place = sum(1 for other in done if other > bit)
        low = jnp.where(mine == 0, block, got)
        high = jnp.where(mine == 0, got, block)
        block = jnp.stack([low, high], axis=place)
        done.append(bit)
    return block.reshape(count, *block.shape[len(bits):])


def on_device(
    image, tv_dual, data_dual, echoes, row_steer, col_steer, kernels, footprint, phase, aperture
):
    highest = lax.Precision.HIGHEST
    az_index = lax.axis_index("az")
    tile_index = lax.axis_index("tile")
    az_count = lax.axis_size("az")
    tile_count = lax.axis_size("tile")
    strip_rows = image.shape[1]
    columns = image.shape[2]
    tiles_dev = row_steer.shape[2]
    tile_rows = row_steer.shape[3]
    rows_dev = data_dual.shape[2]
    range_rows = rows_dev * tile_count
    foot_block = footprint[:, 0, :]
    phase_block = phase[:, 0, :]
    foot_mine = lax.dynamic_slice_in_dim(foot_block, tile_index * tiles_dev, tiles_dev, 0)
    phase_mine = lax.dynamic_slice_in_dim(phase_block, tile_index * tiles_dev, tiles_dev, 0)
    steer_re = row_steer[0]
    steer_im = row_steer[1]
    col_mine = lax.dynamic_slice_in_dim(col_steer, az_index, 1, 3)[..., 0]
    image_b = image.astype(jnp.bfloat16).reshape(2, tiles_dev, tile_rows, columns)
    part_sre = steer_re
    part_sim = steer_im
    weight_re = col_mine[0][..., None]
    weight_im = col_mine[1][..., None]
    prod_re = jnp.einsum("pjh,jhu->pju", part_sre, image_b[0], preferred_element_type=jnp.float32)
    prod_re = prod_re - jnp.einsum(
        "pjh,jhu->pju", part_sim, image_b[1], preferred_element_type=jnp.float32
    )
    prod_im = jnp.einsum("pjh,jhu->pju", part_sre, image_b[1], preferred_element_type=jnp.float32)
    prod_im = prod_im + jnp.einsum(
        "pjh,jhu->pju", part_sim, image_b[0], preferred_element_type=jnp.float32
    )
    real_part = weight_re * prod_re - weight_im * prod_im
    imag_part = weight_re * prod_im + weight_im * prod_re
    parts = jnp.stack([real_part, imag_part], axis=0).reshape(2, az_count, -1, tiles_dev, columns)
    summed = halving_sum(jnp.moveaxis(parts, 1, 0), "az", (1, 8, 2, 4))
    projection_b = jnp.transpose(summed, (2, 1, 0, 3)).astype(jnp.bfloat16)
    tv_image, tv_old, projection_b = lax.optimization_barrier((image, tv_dual, projection_b))
    all_proj = doubling_gather(projection_b, "tile", (2, 1, 8, 4))
    all_proj = all_proj.reshape(-1, *all_proj.shape[2:])
    phase_ids = jnp.arange(kernels.shape[0], dtype=jnp.int32)
    my_rows = tile_index * rows_dev + jnp.arange(rows_dev, dtype=jnp.int32)
    hits = (foot_block[:, :, None, None] == my_rows[None, None, :, None]) & (
        phase_block[:, :, None, None] == phase_ids[None, None, None, :]
    )
    counts = jnp.sum(hits.astype(jnp.int32), axis=1).astype(jnp.bfloat16)
    grouped = jnp.einsum(
        "jkq,jpcu->kqpcu", counts, all_proj, preferred_element_type=jnp.float32
    )
    forward = jnp.einsum(
        "kqpcu,quv->cpkv", grouped, kernels.astype(jnp.float32), precision=highest
    )
    kern_mine = kernels[phase_mine]
    live = (aperture == 1)[None, :, None, None]
    dual_new = jnp.where(
        live,
        (data_dual + dual_step * (forward - echoes.astype(jnp.float32))) / (1.0 + dual_step),
        0.0,
    )
    dual_b = dual_new.astype(jnp.bfloat16)
    all_rows = doubling_gather(jnp.moveaxis(dual_b, 2, 0), "tile", (2, 1, 8, 4))
    all_rows = jnp.moveaxis(all_rows.reshape(-1, *all_rows.shape[2:]), 0, 2)
    row_pick = (foot_mine[:, :, None] == jnp.arange(range_rows, dtype=jnp.int32)).astype(
        jnp.bfloat16
    )
    chosen = jnp.einsum(
        "jfk,cpkv->cpjfv", row_pick, all_rows, preferred_element_type=jnp.float32
    ).astype(jnp.bfloat16)
    back = jnp.einsum("cpjfv,jfuv->cjpu", chosen, kern_mine, preferred_element_type=jnp.float32)
    back_b = back.astype(jnp.bfloat16)
    piece = doubling_gather(jnp.moveaxis(back_b, 2, 0), "az", (4, 8, 2, 1))
    piece = jnp.moveaxis(piece.reshape(-1, *piece.shape[2:]), 0, 2)
    weight_re = col_mine[0].T[..., None]
    weight_im = col_mine[1].T[..., None]
    back_re = piece[0].astype(jnp.float32)
    back_im = piece[1].astype(jnp.float32)
    mixed_re = (weight_re * back_re + weight_im * back_im).astype(jnp.bfloat16)
    mixed_im = (weight_re * back_im - weight_im * back_re).astype(jnp.bfloat16)
    part_sre = steer_re
    part_sim = steer_im
    grad_re = jnp.einsum("pjh,jpu->jhu", part_sre, mixed_re, preferred_element_type=jnp.float32)
    grad_re = grad_re + jnp.einsum(
        "pjh,jpu->jhu", part_sim, mixed_im, preferred_element_type=jnp.float32
    )
    grad_im = jnp.einsum("pjh,jpu->jhu", part_sre, mixed_im, preferred_element_type=jnp.float32)
    grad_im = grad_im - jnp.einsum(
        "pjh,jpu->jhu", part_sim, mixed_re, preferred_element_type=jnp.float32
    )
    adjoint = jnp.stack([grad_re, grad_im])
    adjoint = adjoint.reshape(2, strip_rows, columns)
    total_rows = tile_count * strip_rows
    total_cols = az_count * columns
    global_row = tile_index * strip_rows + jnp.arange(strip_rows, dtype=jnp.int32)
    global_col = az_index * columns + jnp.arange(columns, dtype=jnp.int32)
    last_row = (global_row == total_rows - 1)[None, :, None]
    last_col = (global_col == total_cols - 1)[None, None, :]
    up_tile = [(i + 1, i) for i in range(tile_count - 1)]
    up_az = [(i + 1, i) for i in range(az_count - 1)]
    next_row = lax.ppermute(tv_image[:, :1, :], "tile", up_tile)
    next_col = lax.ppermute(tv_image[:, :, :1], "az", up_az)
    grad_rows = jnp.concatenate([tv_image[:, 1:, :], next_row], axis=1) - tv_image
    grad_rows = jnp.where(last_row, 0.0, grad_rows)
    grad_cols = jnp.concatenate([tv_image[:, :, 1:], next_col], axis=2) - tv_image
    grad_cols = jnp.where(last_col, 0.0, grad_cols)
    moved = tv_old + dual_step * jnp.stack([grad_rows, grad_cols])
    magnitude = jnp.sqrt(jnp.sum(moved * moved, axis=(0, 1)))
    tv_new = moved / jnp.maximum(1.0, magnitude / edge_limit)
    rows_part = jnp.where(last_row, 0.0, tv_new[0])
    cols_part = jnp.where(last_col, 0.0, tv_new[1])
    down_tile = [(i, i + 1) for i in range(tile_count - 1)]
    down_az = [(i, i + 1) for i in range(az_count - 1)]
    prev_row = lax.ppermute(rows_part[:, -1:, :], "tile", down_tile)
    prev_col = lax.ppermute(cols_part[:, :, -1:], "az", down_az)
    divergence = (
        rows_part
        - jnp.concatenate([prev_row, rows_part[:, :-1, :]], axis=1)
        + cols_part
        - jnp.concatenate([prev_col, cols_part[:, :, :-1]], axis=2)
    )
    image_new = image - primal_step * (adjoint - divergence)
    return (image_new, tv_new, dual_new)


def solution(mesh):
    in_specs = (
        P(None, "tile", "az"),
        P(None, None, "tile", "az"),
        P(None, "az", "tile", None),
        P(None, "az", "tile", None),
        P(None, None, "tile", None),
        P(None, None, "tile", None),
        P(),
        P(None, "az", None),
        P(None, "az", None),
        P("az"),
    )
    out_specs = (P(None, "tile", "az"), P(None, None, "tile", "az"), P(None, "az", "tile", None))
    return jax.shard_map(
        on_device, mesh=mesh, in_specs=in_specs, out_specs=out_specs, check_vma=False
    )
```

```python
import jax
import jax.numpy as jnp
from jax import lax
from jax.sharding import PartitionSpec as P

dual_step = 0.5
primal_step = 0.25
edge_limit = 1.5


def padded_2(block, sides, width):
    for axis, dim in sides:
        count = lax.axis_size(axis)
        forward = [(i, i + 1) for i in range(count - 1)]
        backward = [(target, source) for source, target in forward]
        low = lax.ppermute(
            lax.slice_in_dim(block, block.shape[dim] - width, None, axis=dim), axis, forward
        )
        high = lax.ppermute(lax.slice_in_dim(block, 0, width, axis=dim), axis, backward)
        block = jnp.concatenate([low, block, high], axis=dim)
    return block


def halving_sum(blocks, axis, bits):
    me = lax.axis_index(axis)
    count = lax.axis_size(axis)
    order = [count >> (level + 1) for level in range(count.bit_length() - 1)]
    blocks = blocks.reshape(*([2] * len(order)), *blocks.shape[1:])
    for bit in bits:
        place = order.index(bit)
        order.pop(place)
        mine = (me // bit) % 2
        keep = lax.dynamic_index_in_dim(blocks, mine, place, keepdims=False)
        send = lax.dynamic_index_in_dim(blocks, 1 - mine, place, keepdims=False)
        pairs = [(i, i ^ bit) for i in range(count)]
        blocks = keep + lax.ppermute(send, axis, pairs)
    return blocks


def doubling_gather(block, axis, bits):
    me = lax.axis_index(axis)
    count = lax.axis_size(axis)
    done = []
    for bit in bits:
        mine = (me // bit) % 2
        pairs = [(i, i ^ bit) for i in range(count)]
        got = lax.ppermute(block, axis, pairs)
        place = sum(1 for other in done if other > bit)
        low = jnp.where(mine == 0, block, got)
        high = jnp.where(mine == 0, got, block)
        block = jnp.stack([low, high], axis=place)
        done.append(bit)
    return block.reshape(count, *block.shape[len(bits):])


def on_device(
    image, tv_dual, data_dual, echoes, row_steer, col_steer, kernels, footprint, phase, aperture
):
    highest = lax.Precision.HIGHEST
    az_index = lax.axis_index("az")
    tile_index = lax.axis_index("tile")
    az_count = lax.axis_size("az")
    tile_count = lax.axis_size("tile")
    strip_rows = image.shape[1]
    columns = image.shape[2]
    tiles_dev = row_steer.shape[2]
    tile_rows = row_steer.shape[3]
    rows_dev = data_dual.shape[2]
    range_rows = rows_dev * tile_count
    foot_block = footprint[:, 0, :]
    phase_block = phase[:, 0, :]
    foot_mine = lax.dynamic_slice_in_dim(foot_block, tile_index * tiles_dev, tiles_dev, 0)
    phase_mine = lax.dynamic_slice_in_dim(phase_block, tile_index * tiles_dev, tiles_dev, 0)
    steer_re = row_steer[0]
    steer_im = row_steer[1]
    col_mine = lax.dynamic_slice_in_dim(col_steer, az_index, 1, 3)[..., 0]
    image_b = image.astype(jnp.bfloat16).reshape(2, tiles_dev, tile_rows, columns)
    part_sre = jnp.transpose(steer_re, (1, 0, 2))
    part_sim = jnp.transpose(steer_im, (1, 0, 2))
    weight_re = col_mine[0].T[..., None]
    weight_im = col_mine[1].T[..., None]
    prod_re = jnp.einsum("jph,jhu->jpu", part_sre, image_b[0], preferred_element_type=jnp.float32)
    prod_re = prod_re - jnp.einsum(
        "jph,jhu->jpu", part_sim, image_b[1], preferred_element_type=jnp.float32
    )
    prod_im = jnp.einsum("jph,jhu->jpu", part_sre, image_b[1], preferred_element_type=jnp.float32)
    prod_im = prod_im + jnp.einsum(
        "jph,jhu->jpu", part_sim, image_b[0], preferred_element_type=jnp.float32
    )
    real_part = jnp.transpose(weight_re * prod_re - weight_im * prod_im, (1, 0, 2))
    imag_part = jnp.transpose(weight_re * prod_im + weight_im * prod_re, (1, 0, 2))
    parts = jnp.stack([real_part, imag_part], axis=0).reshape(2, az_count, -1, tiles_dev, columns)
    summed = halving_sum(jnp.moveaxis(parts, 1, 0), "az", (1, 8, 2, 4))
    projection_b = jnp.transpose(summed, (2, 1, 0, 3)).astype(jnp.bfloat16)
    all_proj = doubling_gather(projection_b, "tile", (2, 1, 8, 4))
    all_proj = all_proj.reshape(-1, *all_proj.shape[2:])
    phase_ids = jnp.arange(kernels.shape[0], dtype=jnp.int32)
    my_rows = tile_index * rows_dev + jnp.arange(rows_dev, dtype=jnp.int32)
    hits = (foot_block[:, :, None, None] == my_rows[None, None, :, None]) & (
        phase_block[:, :, None, None] == phase_ids[None, None, None, :]
    )
    counts = jnp.sum(hits.astype(jnp.int32), axis=1).astype(jnp.bfloat16)
    grouped = jnp.einsum(
        "jkq,jpcu->kqpcu", counts, all_proj, preferred_element_type=jnp.float32
    )
    forward = jnp.einsum(
        "kqpcu,quv->cpkv", grouped, kernels.astype(jnp.float32), precision=highest
    )
    kern_mine = kernels[phase_mine]
    live = (aperture == 1)[None, :, None, None]
    dual_new = jnp.where(
        live,
        (data_dual + dual_step * (forward - echoes.astype(jnp.float32))) / (1.0 + dual_step),
        0.0,
    )
    dual_b = dual_new.astype(jnp.bfloat16)
    all_rows = doubling_gather(jnp.moveaxis(dual_b, 2, 0), "tile", (2, 1, 8, 4))
    all_rows = jnp.moveaxis(all_rows.reshape(-1, *all_rows.shape[2:]), 0, 2)
    row_pick = (foot_mine[:, :, None] == jnp.arange(range_rows, dtype=jnp.int32)).astype(
        jnp.bfloat16
    )
    chosen = jnp.einsum(
        "jfk,cpkv->cpjfv", row_pick, all_rows, preferred_element_type=jnp.float32
    ).astype(jnp.bfloat16)
    back = jnp.einsum("cpjfv,jfuv->cjpu", chosen, kern_mine, preferred_element_type=jnp.float32)
    back_b = back.astype(jnp.bfloat16)
    piece = doubling_gather(jnp.moveaxis(back_b, 2, 0), "az", (4, 8, 2, 1))
    piece = jnp.moveaxis(piece.reshape(-1, *piece.shape[2:]), 0, 2)
    weight_re = col_mine[0].T[..., None]
    weight_im = col_mine[1].T[..., None]
    back_re = piece[0].astype(jnp.float32)
    back_im = piece[1].astype(jnp.float32)
    mixed_re = (weight_re * back_re + weight_im * back_im).astype(jnp.bfloat16)
    mixed_im = (weight_re * back_im - weight_im * back_re).astype(jnp.bfloat16)
    part_sre = steer_re
    part_sim = steer_im
    grad_re = jnp.einsum("pjh,jpu->jhu", part_sre, mixed_re, preferred_element_type=jnp.float32)
    grad_re = grad_re + jnp.einsum(
        "pjh,jpu->jhu", part_sim, mixed_im, preferred_element_type=jnp.float32
    )
    grad_im = jnp.einsum("pjh,jpu->jhu", part_sre, mixed_im, preferred_element_type=jnp.float32)
    grad_im = grad_im - jnp.einsum(
        "pjh,jpu->jhu", part_sim, mixed_re, preferred_element_type=jnp.float32
    )
    adjoint = jnp.stack([grad_re, grad_im])
    adjoint = adjoint.reshape(2, strip_rows, columns)
    stacked = jnp.concatenate([image, tv_dual.reshape(4, strip_rows, columns)], axis=0)
    padded = padded_2(stacked, (("az", 2), ("tile", 1)), 1)
    image_pad = padded[:2]
    dual_pad = padded[2:].reshape(2, 2, strip_rows + 2, columns + 2)
    total_rows = tile_count * strip_rows
    total_cols = az_count * columns
    global_row = tile_index * strip_rows - 1 + jnp.arange(strip_rows + 1, dtype=jnp.int32)
    global_col = az_index * columns - 1 + jnp.arange(columns + 1, dtype=jnp.int32)
    centre = image_pad[:, : strip_rows + 1, : columns + 1]
    grad_rows = image_pad[:, 1 : strip_rows + 2, : columns + 1] - centre
    grad_rows = jnp.where((global_row < total_rows - 1)[None, :, None], grad_rows, 0.0)
    grad_cols = image_pad[:, : strip_rows + 1, 1 : columns + 2] - centre
    grad_cols = jnp.where((global_col < total_cols - 1)[None, None, :], grad_cols, 0.0)
    moved = dual_pad[:, :, : strip_rows + 1, : columns + 1] + dual_step * jnp.stack(
        [grad_rows, grad_cols]
    )
    magnitude = jnp.sqrt(jnp.sum(moved * moved, axis=(0, 1)))
    projected = moved / jnp.maximum(1.0, magnitude / edge_limit)
    inside = (global_row >= 0)[:, None] & (global_col >= 0)[None, :]
    projected = jnp.where(inside[None, None], projected, 0.0)
    rows_part = jnp.where((global_row < total_rows - 1)[None, :, None], projected[0], 0.0)
    cols_part = jnp.where((global_col < total_cols - 1)[None, None, :], projected[1], 0.0)
    divergence = (
        rows_part[:, 1:, 1:] - rows_part[:, :-1, 1:] + cols_part[:, 1:, 1:] - cols_part[:, 1:, :-1]
    )
    image_new = image - primal_step * (adjoint - divergence)
    tv_new = projected[:, :, 1:, 1:]
    return (image_new, tv_new, dual_new)


def solution(mesh):
    in_specs = (
        P(None, "tile", "az"),
        P(None, None, "tile", "az"),
        P(None, "az", "tile", None),
        P(None, "az", "tile", None),
        P(None, None, "tile", None),
        P(None, None, "tile", None),
        P(),
        P(None, "az", None),
        P(None, "az", None),
        P("az"),
    )
    out_specs = (P(None, "tile", "az"), P(None, None, "tile", "az"), P(None, "az", "tile", None))
    return jax.shard_map(
        on_device, mesh=mesh, in_specs=in_specs, out_specs=out_specs, check_vma=False
    )
```

```python
import jax
import jax.numpy as jnp
from jax import lax
from jax.sharding import PartitionSpec as P

dual_step = 0.5
primal_step = 0.25
edge_limit = 1.5


def padded_2(block, sides, width):
    for axis, dim in sides:
        count = lax.axis_size(axis)
        forward = [(i, i + 1) for i in range(count - 1)]
        backward = [(target, source) for source, target in forward]
        low = lax.ppermute(
            lax.slice_in_dim(block, block.shape[dim] - width, None, axis=dim), axis, forward
        )
        high = lax.ppermute(lax.slice_in_dim(block, 0, width, axis=dim), axis, backward)
        block = jnp.concatenate([low, block, high], axis=dim)
    return block


def halving_sum(blocks, axis, bits):
    me = lax.axis_index(axis)
    count = lax.axis_size(axis)
    order = [count >> (level + 1) for level in range(count.bit_length() - 1)]
    blocks = blocks.reshape(*([2] * len(order)), *blocks.shape[1:])
    for bit in bits:
        place = order.index(bit)
        order.pop(place)
        mine = (me // bit) % 2
        keep = lax.dynamic_index_in_dim(blocks, mine, place, keepdims=False)
        send = lax.dynamic_index_in_dim(blocks, 1 - mine, place, keepdims=False)
        pairs = [(i, i ^ bit) for i in range(count)]
        blocks = keep + lax.ppermute(send, axis, pairs)
    return blocks


def doubling_gather(block, axis, bits):
    me = lax.axis_index(axis)
    count = lax.axis_size(axis)
    done = []
    for bit in bits:
        mine = (me // bit) % 2
        pairs = [(i, i ^ bit) for i in range(count)]
        got = lax.ppermute(block, axis, pairs)
        place = sum(1 for other in done if other > bit)
        low = jnp.where(mine == 0, block, got)
        high = jnp.where(mine == 0, got, block)
        block = jnp.stack([low, high], axis=place)
        done.append(bit)
    return block.reshape(count, *block.shape[len(bits):])


def on_device(
    image, tv_dual, data_dual, echoes, row_steer, col_steer, kernels, footprint, phase, aperture
):
    highest = lax.Precision.HIGHEST
    az_index = lax.axis_index("az")
    tile_index = lax.axis_index("tile")
    az_count = lax.axis_size("az")
    tile_count = lax.axis_size("tile")
    strip_rows = image.shape[1]
    columns = image.shape[2]
    tiles_dev = row_steer.shape[2]
    tile_rows = row_steer.shape[3]
    rows_dev = data_dual.shape[2]
    range_rows = rows_dev * tile_count
    foot_block = footprint[:, 0, :]
    phase_block = phase[:, 0, :]
    foot_mine = lax.dynamic_slice_in_dim(foot_block, tile_index * tiles_dev, tiles_dev, 0)
    phase_mine = lax.dynamic_slice_in_dim(phase_block, tile_index * tiles_dev, tiles_dev, 0)
    steer_re = row_steer[0]
    steer_im = row_steer[1]
    col_mine = lax.dynamic_slice_in_dim(col_steer, az_index, 1, 3)[..., 0]
    image_b = image.astype(jnp.bfloat16).reshape(2, tiles_dev, tile_rows, columns)
    part_sre = jnp.transpose(steer_re, (1, 0, 2))
    part_sim = jnp.transpose(steer_im, (1, 0, 2))
    weight_re = col_mine[0].T[..., None]
    weight_im = col_mine[1].T[..., None]
    prod_re = jnp.einsum("jph,jhu->jpu", part_sre, image_b[0], preferred_element_type=jnp.float32)
    prod_re = prod_re - jnp.einsum(
        "jph,jhu->jpu", part_sim, image_b[1], preferred_element_type=jnp.float32
    )
    prod_im = jnp.einsum("jph,jhu->jpu", part_sre, image_b[1], preferred_element_type=jnp.float32)
    prod_im = prod_im + jnp.einsum(
        "jph,jhu->jpu", part_sim, image_b[0], preferred_element_type=jnp.float32
    )
    real_part = jnp.transpose(weight_re * prod_re - weight_im * prod_im, (1, 0, 2))
    imag_part = jnp.transpose(weight_re * prod_im + weight_im * prod_re, (1, 0, 2))
    parts = jnp.stack([real_part, imag_part], axis=0).reshape(2, az_count, -1, tiles_dev, columns)
    summed = halving_sum(jnp.moveaxis(parts, 1, 0), "az", (1, 8, 2, 4))
    projection_b = jnp.transpose(summed, (2, 1, 0, 3)).astype(jnp.bfloat16)
    all_proj = doubling_gather(projection_b, "tile", (2, 1, 8, 4))
    all_proj = all_proj.reshape(-1, *all_proj.shape[2:])
    phase_ids = jnp.arange(kernels.shape[0], dtype=jnp.int32)
    my_rows = tile_index * rows_dev + jnp.arange(rows_dev, dtype=jnp.int32)
    hits = (foot_block[:, :, None, None] == my_rows[None, None, :, None]) & (
        phase_block[:, :, None, None] == phase_ids[None, None, None, :]
    )
    counts = jnp.sum(hits.astype(jnp.int32), axis=1).astype(jnp.bfloat16)
    grouped = jnp.einsum(
        "jkq,jpcu->kqpcu", counts, all_proj, preferred_element_type=jnp.float32
    )
    grouped_hi = grouped.astype(jnp.bfloat16)
    rest = grouped - grouped_hi.astype(jnp.float32)
    grouped_mid = rest.astype(jnp.bfloat16)
    grouped_lo = (rest - grouped_mid.astype(jnp.float32)).astype(jnp.bfloat16)
    forward = sum(
        jnp.einsum("kqpcu,quv->cpkv", piece, kernels, preferred_element_type=jnp.float32)
        for piece in (grouped_lo, grouped_mid, grouped_hi)
    )
    kern_mine = kernels[phase_mine]
    live = (aperture == 1)[None, :, None, None]
    dual_new = jnp.where(
        live,
        (data_dual + dual_step * (forward - echoes.astype(jnp.float32))) / (1.0 + dual_step),
        0.0,
    )
    dual_b = dual_new.astype(jnp.bfloat16)
    all_rows = doubling_gather(jnp.moveaxis(dual_b, 2, 0), "tile", (2, 1, 8, 4))
    all_rows = jnp.moveaxis(all_rows.reshape(-1, *all_rows.shape[2:]), 0, 2)
    row_pick = (foot_mine[:, :, None] == jnp.arange(range_rows, dtype=jnp.int32)).astype(
        jnp.bfloat16
    )
    chosen = jnp.einsum(
        "jfk,cpkv->cpjfv", row_pick, all_rows, preferred_element_type=jnp.float32
    ).astype(jnp.bfloat16)
    back = jnp.einsum("cpjfv,jfuv->cjpu", chosen, kern_mine, preferred_element_type=jnp.float32)
    back_b = back.astype(jnp.bfloat16)
    piece = doubling_gather(jnp.moveaxis(back_b, 2, 0), "az", (4, 8, 2, 1))
    piece = jnp.moveaxis(piece.reshape(-1, *piece.shape[2:]), 0, 2)
    weight_re = col_mine[0].T[..., None]
    weight_im = col_mine[1].T[..., None]
    back_re = piece[0].astype(jnp.float32)
    back_im = piece[1].astype(jnp.float32)
    mixed_re = (weight_re * back_re + weight_im * back_im).astype(jnp.bfloat16)
    mixed_im = (weight_re * back_im - weight_im * back_re).astype(jnp.bfloat16)
    part_sre = steer_re
    part_sim = steer_im
    grad_re = jnp.einsum("pjh,jpu->jhu", part_sre, mixed_re, preferred_element_type=jnp.float32)
    grad_re = grad_re + jnp.einsum(
        "pjh,jpu->jhu", part_sim, mixed_im, preferred_element_type=jnp.float32
    )
    grad_im = jnp.einsum("pjh,jpu->jhu", part_sre, mixed_im, preferred_element_type=jnp.float32)
    grad_im = grad_im - jnp.einsum(
        "pjh,jpu->jhu", part_sim, mixed_re, preferred_element_type=jnp.float32
    )
    adjoint = jnp.stack([grad_re, grad_im])
    adjoint = adjoint.reshape(2, strip_rows, columns)
    stacked = jnp.concatenate([image, tv_dual.reshape(4, strip_rows, columns)], axis=0)
    padded = padded_2(stacked, (("az", 2), ("tile", 1)), 1)
    image_pad = padded[:2]
    dual_pad = padded[2:].reshape(2, 2, strip_rows + 2, columns + 2)
    total_rows = tile_count * strip_rows
    total_cols = az_count * columns
    global_row = tile_index * strip_rows - 1 + jnp.arange(strip_rows + 1, dtype=jnp.int32)
    global_col = az_index * columns - 1 + jnp.arange(columns + 1, dtype=jnp.int32)
    centre = image_pad[:, : strip_rows + 1, : columns + 1]
    grad_rows = image_pad[:, 1 : strip_rows + 2, : columns + 1] - centre
    grad_rows = jnp.where((global_row < total_rows - 1)[None, :, None], grad_rows, 0.0)
    grad_cols = image_pad[:, : strip_rows + 1, 1 : columns + 2] - centre
    grad_cols = jnp.where((global_col < total_cols - 1)[None, None, :], grad_cols, 0.0)
    moved = dual_pad[:, :, : strip_rows + 1, : columns + 1] + dual_step * jnp.stack(
        [grad_rows, grad_cols]
    )
    magnitude = jnp.sqrt(jnp.sum(moved * moved, axis=(0, 1)))
    projected = moved / jnp.maximum(1.0, magnitude / edge_limit)
    inside = (global_row >= 0)[:, None] & (global_col >= 0)[None, :]
    projected = jnp.where(inside[None, None], projected, 0.0)
    rows_part = jnp.where((global_row < total_rows - 1)[None, :, None], projected[0], 0.0)
    cols_part = jnp.where((global_col < total_cols - 1)[None, None, :], projected[1], 0.0)
    divergence = (
        rows_part[:, 1:, 1:] - rows_part[:, :-1, 1:] + cols_part[:, 1:, 1:] - cols_part[:, 1:, :-1]
    )
    image_new = image - primal_step * (adjoint - divergence)
    tv_new = projected[:, :, 1:, 1:]
    return (image_new, tv_new, dual_new)


def solution(mesh):
    in_specs = (
        P(None, "tile", "az"),
        P(None, None, "tile", "az"),
        P(None, "az", "tile", None),
        P(None, "az", "tile", None),
        P(None, None, "tile", None),
        P(None, None, "tile", None),
        P(),
        P(None, "az", None),
        P(None, "az", None),
        P("az"),
    )
    out_specs = (P(None, "tile", "az"), P(None, None, "tile", "az"), P(None, "az", "tile", None))
    return jax.shard_map(
        on_device, mesh=mesh, in_specs=in_specs, out_specs=out_specs, check_vma=False
    )
```

```python
import jax
import jax.numpy as jnp
from jax import lax
from jax.sharding import PartitionSpec as P

dual_step = 0.5
primal_step = 0.25
edge_limit = 1.5


def padded_2(block, sides, width):
    for axis, dim in sides:
        count = lax.axis_size(axis)
        forward = [(i, i + 1) for i in range(count - 1)]
        backward = [(target, source) for source, target in forward]
        low = lax.ppermute(
            lax.slice_in_dim(block, block.shape[dim] - width, None, axis=dim), axis, forward
        )
        high = lax.ppermute(lax.slice_in_dim(block, 0, width, axis=dim), axis, backward)
        block = jnp.concatenate([low, block, high], axis=dim)
    return block


def halving_sum(blocks, axis, bits):
    me = lax.axis_index(axis)
    count = lax.axis_size(axis)
    order = [count >> (level + 1) for level in range(count.bit_length() - 1)]
    blocks = blocks.reshape(*([2] * len(order)), *blocks.shape[1:])
    for bit in bits:
        place = order.index(bit)
        order.pop(place)
        mine = (me // bit) % 2
        keep = lax.dynamic_index_in_dim(blocks, mine, place, keepdims=False)
        send = lax.dynamic_index_in_dim(blocks, 1 - mine, place, keepdims=False)
        pairs = [(i, i ^ bit) for i in range(count)]
        blocks = keep + lax.ppermute(send, axis, pairs)
    return blocks


def doubling_gather(block, axis, bits):
    me = lax.axis_index(axis)
    count = lax.axis_size(axis)
    done = []
    for bit in bits:
        mine = (me // bit) % 2
        pairs = [(i, i ^ bit) for i in range(count)]
        got = lax.ppermute(block, axis, pairs)
        place = sum(1 for other in done if other > bit)
        low = jnp.where(mine == 0, block, got)
        high = jnp.where(mine == 0, got, block)
        block = jnp.stack([low, high], axis=place)
        done.append(bit)
    return block.reshape(count, *block.shape[len(bits):])


def on_device(
    image, tv_dual, data_dual, echoes, row_steer, col_steer, kernels, footprint, phase, aperture
):
    highest = lax.Precision.HIGHEST
    az_index = lax.axis_index("az")
    tile_index = lax.axis_index("tile")
    az_count = lax.axis_size("az")
    tile_count = lax.axis_size("tile")
    strip_rows = image.shape[1]
    columns = image.shape[2]
    tiles_dev = row_steer.shape[2]
    tile_rows = row_steer.shape[3]
    rows_dev = data_dual.shape[2]
    range_rows = rows_dev * tile_count
    foot_block = footprint[:, 0, :]
    phase_block = phase[:, 0, :]
    foot_mine = lax.dynamic_slice_in_dim(foot_block, tile_index * tiles_dev, tiles_dev, 0)
    phase_mine = lax.dynamic_slice_in_dim(phase_block, tile_index * tiles_dev, tiles_dev, 0)
    steer_re = row_steer[0]
    steer_im = row_steer[1]
    col_pick = jnp.arange(col_steer.shape[3], dtype=jnp.int32) == az_index
    col_mine = jnp.sum(jnp.where(col_pick, col_steer, 0.0), axis=3)
    image_b = image.astype(jnp.bfloat16).reshape(2, tiles_dev, tile_rows, columns)
    part_sre = jnp.transpose(steer_re, (1, 0, 2))
    part_sim = jnp.transpose(steer_im, (1, 0, 2))
    weight_re = col_mine[0].T[..., None]
    weight_im = col_mine[1].T[..., None]
    prod_re = jnp.einsum("jph,jhu->jpu", part_sre, image_b[0], preferred_element_type=jnp.float32)
    prod_re = prod_re - jnp.einsum(
        "jph,jhu->jpu", part_sim, image_b[1], preferred_element_type=jnp.float32
    )
    prod_im = jnp.einsum("jph,jhu->jpu", part_sre, image_b[1], preferred_element_type=jnp.float32)
    prod_im = prod_im + jnp.einsum(
        "jph,jhu->jpu", part_sim, image_b[0], preferred_element_type=jnp.float32
    )
    real_part = jnp.transpose(weight_re * prod_re - weight_im * prod_im, (1, 0, 2))
    imag_part = jnp.transpose(weight_re * prod_im + weight_im * prod_re, (1, 0, 2))
    parts = jnp.stack([real_part, imag_part], axis=0).reshape(2, az_count, -1, tiles_dev, columns)
    summed = halving_sum(jnp.moveaxis(parts, 1, 0), "az", (1, 8, 2, 4))
    projection_b = jnp.transpose(summed, (2, 1, 0, 3)).astype(jnp.bfloat16)
    all_proj = doubling_gather(projection_b, "tile", (2, 1, 8, 4))
    all_proj = all_proj.reshape(-1, *all_proj.shape[2:])
    phase_ids = jnp.arange(kernels.shape[0], dtype=jnp.int32)
    my_rows = tile_index * rows_dev + jnp.arange(rows_dev, dtype=jnp.int32)
    hits = (foot_block[:, :, None, None] == my_rows[None, None, :, None]) & (
        phase_block[:, :, None, None] == phase_ids[None, None, None, :]
    )
    counts = jnp.sum(hits.astype(jnp.int32), axis=1).astype(jnp.bfloat16)
    grouped = jnp.einsum(
        "jkq,jpcu->kqpcu", counts, all_proj, preferred_element_type=jnp.float32
    )
    forward = jnp.einsum(
        "kqpcu,quv->cpkv", grouped, kernels.astype(jnp.float32), precision=highest
    )
    kern_mine = kernels[phase_mine]
    live = (aperture == 1)[None, :, None, None]
    dual_new = jnp.where(
        live,
        (data_dual + dual_step * (forward - echoes.astype(jnp.float32))) / (1.0 + dual_step),
        0.0,
    )
    dual_b = dual_new.astype(jnp.bfloat16)
    all_rows = doubling_gather(jnp.moveaxis(dual_b, 2, 0), "tile", (2, 1, 8, 4))
    all_rows = jnp.moveaxis(all_rows.reshape(-1, *all_rows.shape[2:]), 0, 2)
    row_pick = (foot_mine[:, :, None] == jnp.arange(range_rows, dtype=jnp.int32)).astype(
        jnp.bfloat16
    )
    chosen = jnp.einsum(
        "jfk,cpkv->cpjfv", row_pick, all_rows, preferred_element_type=jnp.float32
    ).astype(jnp.bfloat16)
    back = jnp.einsum("cpjfv,jfuv->cjpu", chosen, kern_mine, preferred_element_type=jnp.float32)
    back_b = back.astype(jnp.bfloat16)
    piece = doubling_gather(jnp.moveaxis(back_b, 2, 0), "az", (4, 8, 2, 1))
    piece = jnp.moveaxis(piece.reshape(-1, *piece.shape[2:]), 0, 2)
    weight_re = col_mine[0].T[..., None]
    weight_im = col_mine[1].T[..., None]
    back_re = piece[0].astype(jnp.float32)
    back_im = piece[1].astype(jnp.float32)
    mixed_re = (weight_re * back_re + weight_im * back_im).astype(jnp.bfloat16)
    mixed_im = (weight_re * back_im - weight_im * back_re).astype(jnp.bfloat16)
    part_sre = steer_re
    part_sim = steer_im
    grad_re = jnp.einsum("pjh,jpu->jhu", part_sre, mixed_re, preferred_element_type=jnp.float32)
    grad_re = grad_re + jnp.einsum(
        "pjh,jpu->jhu", part_sim, mixed_im, preferred_element_type=jnp.float32
    )
    grad_im = jnp.einsum("pjh,jpu->jhu", part_sre, mixed_im, preferred_element_type=jnp.float32)
    grad_im = grad_im - jnp.einsum(
        "pjh,jpu->jhu", part_sim, mixed_re, preferred_element_type=jnp.float32
    )
    adjoint = jnp.stack([grad_re, grad_im])
    adjoint = adjoint.reshape(2, strip_rows, columns)
    stacked = jnp.concatenate([image, tv_dual.reshape(4, strip_rows, columns)], axis=0)
    padded = padded_2(stacked, (("az", 2), ("tile", 1)), 1)
    image_pad = padded[:2]
    dual_pad = padded[2:].reshape(2, 2, strip_rows + 2, columns + 2)
    total_rows = tile_count * strip_rows
    total_cols = az_count * columns
    global_row = tile_index * strip_rows - 1 + jnp.arange(strip_rows + 1, dtype=jnp.int32)
    global_col = az_index * columns - 1 + jnp.arange(columns + 1, dtype=jnp.int32)
    centre = image_pad[:, : strip_rows + 1, : columns + 1]
    grad_rows = image_pad[:, 1 : strip_rows + 2, : columns + 1] - centre
    grad_rows = jnp.where((global_row < total_rows - 1)[None, :, None], grad_rows, 0.0)
    grad_cols = image_pad[:, : strip_rows + 1, 1 : columns + 2] - centre
    grad_cols = jnp.where((global_col < total_cols - 1)[None, None, :], grad_cols, 0.0)
    moved = dual_pad[:, :, : strip_rows + 1, : columns + 1] + dual_step * jnp.stack(
        [grad_rows, grad_cols]
    )
    magnitude = jnp.sqrt(jnp.sum(moved * moved, axis=(0, 1)))
    projected = moved / jnp.maximum(1.0, magnitude / edge_limit)
    inside = (global_row >= 0)[:, None] & (global_col >= 0)[None, :]
    projected = jnp.where(inside[None, None], projected, 0.0)
    rows_part = jnp.where((global_row < total_rows - 1)[None, :, None], projected[0], 0.0)
    cols_part = jnp.where((global_col < total_cols - 1)[None, None, :], projected[1], 0.0)
    divergence = (
        rows_part[:, 1:, 1:] - rows_part[:, :-1, 1:] + cols_part[:, 1:, 1:] - cols_part[:, 1:, :-1]
    )
    image_new = image - primal_step * (adjoint - divergence)
    tv_new = projected[:, :, 1:, 1:]
    return (image_new, tv_new, dual_new)


def solution(mesh):
    in_specs = (
        P(None, "tile", "az"),
        P(None, None, "tile", "az"),
        P(None, "az", "tile", None),
        P(None, "az", "tile", None),
        P(None, None, "tile", None),
        P(None, None, "tile", None),
        P(),
        P(None, "az", None),
        P(None, "az", None),
        P("az"),
    )
    out_specs = (P(None, "tile", "az"), P(None, None, "tile", "az"), P(None, "az", "tile", None))
    return jax.shard_map(
        on_device, mesh=mesh, in_specs=in_specs, out_specs=out_specs, check_vma=False
    )
```
